256 devices in a mesh: ctx: 64 (over z, y_hi, x), tp: 4 (over y_lo, core).
Axes of the slice: x: 4, y: 4 (y_hi: 2, y_lo: 2; y = y_hi * 2 + y_lo), z: 8, core: 2. Of those that a mesh axis runs over, the one named last changes fastest.
Arguments:
- query_in: bfloat16 [2048, 8192], P('tp', 'ctx'), may hold values from -6 to 6
- key_in: bfloat16 [2048, 8192], P('tp', 'ctx'), may hold values from -6 to 6
- value_in: bfloat16 [2048, 8192], P('tp', 'ctx'), may hold values from -6 to 6
- short_weights: float32 [3, 2048, 7], P(None, 'tp'), may hold values from -3 to 3
- filters: float32 [4, 512, 8192], P('tp', 'ctx'), may hold values from 0 to 1
- out_weight: bfloat16 [4096, 2048], P(None, 'tp'), may hold values from -0.125 to 0.125
- cotangent: bfloat16 [4096, 8192], P('tp', 'ctx'), may hold values from -16 to 16
Outputs:
- mixed_out: bfloat16 [4096, 8192], P('tp', 'ctx')
- grad_query: bfloat16 [2048, 8192], P('tp', 'ctx')
- grad_key: bfloat16 [2048, 8192], P('tp', 'ctx')
- grad_value: bfloat16 [2048, 8192], P('tp', 'ctx')
- grad_filters: float32 [4, 512, 8192], P('tp', 'ctx')
- grad_out_weight: float32 [4096, 2048], P('ctx', 'tp')
The draws below stay inside these ranges and needn't reach their ends.
All inputs are finite; a program needn't handle non-finite values.
Results may differ from the reference program's by a relative error of at most 0.012.
Values may be sent and summed in bfloat16 or wider, within the bound.
No kernel may reach another device: no remote copies, remote signals or barrier semaphores. Data moves between devices by JAX's collectives and lax.ppermute only.
A program may use at most 128 MiB of HBM per device.

```python
import math
import jax
import jax.numpy as jnp

D = 4096
C = 2048
TAPS = 7
CONTEXT_SPAN = 8192
TPG = 4
CT = 512


def draw_filters(key, part):
    lookup_fragments = jax.random.split(jax.random.fold_in(key, 11), 5)
    shape = (TPG, CT, CONTEXT_SPAN)
    element_indices = jnp.arange(CONTEXT_SPAN, dtype=jnp.float32)
    chooser = jax.random.uniform(lookup_fragments[0], (TPG, CT, 1), jnp.float32)
    slow_mask = chooser < 0.5
    rough = jax.random.uniform(lookup_fragments[4], shape, jnp.float32, 0.4, 1.6)
    slow_rate = jnp.exp(jax.random.uniform(lookup_fragments[1], (TPG, CT, 1), jnp.float32, math.log(0.3 / CONTEXT_SPAN), math.log(2.0 / CONTEXT_SPAN)))
    fast_rate = jnp.exp(jax.random.uniform(lookup_fragments[2], (TPG, CT, 1), jnp.float32, math.log(1.0 / 60.0), math.log(1.0 / 20.0)))
    rate = jnp.where(slow_mask, slow_rate, fast_rate)
    cluster_batches = jax.random.randint(lookup_fragments[3], (3,), 1, CONTEXT_SPAN).astype(jnp.float32)
    discarded_entries = jnp.ones((CONTEXT_SPAN,), jnp.float32)
    for chosen_portion in range(3):
        discarded_entries = discarded_entries * jnp.where(element_indices >= cluster_batches[chosen_portion], 0.6, 1.0)
    amplitude = jnp.sqrt(2.0 * rate)
    return amplitude * jnp.exp(-rate * element_indices) * discarded_entries * rough


def spiked(values, own_key, source, target, shards_of, factor):
    owner, partner = [(jnp.arange(values.shape[axis_at]) // (values.shape[axis_at] // shards_of)).reshape([-1 if axis == axis_at else 1 for axis in range(values.ndim)]) for axis_at in (source, target)]
    chosen = jax.random.permutation(own_key, shards_of)[partner]
    strong = (owner == chosen) | (owner == (partner + shards_of // 2) % shards_of)
    return jnp.where(strong, factor * values, values)


def level_of(rng, shape, shards, smallest, top_value):
    gain = 1.0
    for position, parts in shards:
        heights = jax.random.uniform(jax.random.fold_in(jax.random.fold_in(rng, 6), position), (parts,), jnp.float32, smallest / len(shards), top_value / len(shards))
        gain = gain * jnp.repeat(jnp.exp(heights), shape[position] // parts).reshape((-1,) + (1,) * (len(shape) - 1 - position))
    return gain


def scatter_about(own_key, dims, spread, most, cuts=(), held_as=jnp.bfloat16):
    gain = level_of(own_key, dims, cuts, -0.22, 0.18) if cuts else 1.0
    values = jax.random.normal(own_key, dims, jnp.float32) * spread * gain
    return jnp.minimum(jnp.maximum(values, -most), most).astype(held_as)


def heavy_noise(key, extent, deviation, reach, cuts, heavy, kind=jnp.bfloat16):
    array = deviation * jax.random.normal(key, extent, jnp.float32)
    if cuts:
        array = array * level_of(key, extent, cuts, -0.22, 0.18)
    return jnp.clip(spiked(array, jax.random.fold_in(key, 3), *heavy), -reach, reach).astype(kind)


def setup_inputs(seed: int = 0) -> dict:
    streams_of = jax.random.split(jax.random.key(seed), 8)
    query_in = scatter_about(streams_of[0], (C, CONTEXT_SPAN), 1.0, 6.0, ((0, 4), (1, 64)))
    key_in = scatter_about(streams_of[1], (C, CONTEXT_SPAN), 1.0, 6.0, ((0, 4), (1, 64)))
    value_in = scatter_about(streams_of[2], (C, CONTEXT_SPAN), 1.0, 6.0, ((0, 4), (1, 64)))
    short_weights = scatter_about(streams_of[3], (3, C, TAPS), 0.4, 3.0, ((1, 4),), jnp.float32)
    filters = draw_filters(jax.random.fold_in(streams_of[7], 71), 0)
    out_weight = scatter_about(streams_of[5], (D, C), C ** -0.5, 0.125, ((1, 4),))
    cotangent = heavy_noise(streams_of[6], (D, CONTEXT_SPAN), 1.0, 16.0, ((0, 4), (1, 64)), (1, 0, 64, 4.0))
    return {"query_in": query_in, "key_in": key_in, "value_in": value_in, "short_weights": short_weights, "filters": filters, "out_weight": out_weight, "cotangent": cotangent}


def causal_taps(stacked, weights):
    tap_count = weights.shape[2]
    length = stacked.shape[2]
    padded = jnp.pad(stacked.astype(jnp.float32), ((0, 0), (0, 0), (tap_count - 1, 0)))
    running_total = jnp.zeros(stacked.shape, jnp.float32)
    for offset in range(tap_count):
        begin = tap_count - 1 - offset
        running_total = running_total + weights[:, :, offset:offset + 1] * padded[:, :, begin:begin + length]
    return running_total


def anticausal_taps(stacked, weights):
    tap_count = weights.shape[2]
    length = stacked.shape[2]
    padded = jnp.pad(stacked.astype(jnp.float32), ((0, 0), (0, 0), (0, tap_count - 1)))
    running_total = jnp.zeros(stacked.shape, jnp.float32)
    for offset in range(tap_count):
        running_total = running_total + weights[:, :, offset:offset + 1] * padded[:, :, offset:offset + length]
    return running_total


def reference(query_in, key_in, value_in, short_weights, filters, out_weight, cotangent):
    full_len = 2 * CONTEXT_SPAN
    shorts = causal_taps(jnp.stack([query_in, key_in, value_in]), short_weights).astype(jnp.bfloat16)
    product = (shorts[1].astype(jnp.float32) * shorts[2].astype(jnp.float32)).astype(jnp.bfloat16)
    kernel = filters.reshape(C, CONTEXT_SPAN)
    kernel_spec = jnp.fft.rfft(kernel, n=full_len, axis=1)
    product_spec = jnp.fft.rfft(product.astype(jnp.float32), n=full_len, axis=1)
    convolved = jnp.fft.irfft(product_spec * kernel_spec, n=full_len, axis=1)[:, :CONTEXT_SPAN].astype(jnp.bfloat16)
    gated_out = (shorts[0].astype(jnp.float32) * convolved.astype(jnp.float32)).astype(jnp.bfloat16)
    mixed_out = jnp.dot(out_weight, gated_out, preferred_element_type=jnp.float32).astype(jnp.bfloat16)
    grad_gated = jnp.dot(out_weight.T, cotangent, preferred_element_type=jnp.float32)
    grad_out_weight = jnp.dot(cotangent, gated_out.T, preferred_element_type=jnp.float32)
    grad_conv = (grad_gated * shorts[0].astype(jnp.float32)).astype(jnp.bfloat16)
    grad_spec = jnp.fft.rfft(grad_conv.astype(jnp.float32), n=full_len, axis=1)
    derivative_of_multiple = jnp.fft.irfft(jnp.conj(kernel_spec) * grad_spec, n=full_len, axis=1)[:, :CONTEXT_SPAN].astype(jnp.bfloat16)
    grad_filters = jnp.fft.irfft(jnp.conj(product_spec) * grad_spec, n=full_len, axis=1)[:, :CONTEXT_SPAN].reshape(filters.shape)
    grad_shorts = jnp.stack([
        grad_gated * convolved.astype(jnp.float32),
        derivative_of_multiple.astype(jnp.float32) * shorts[2].astype(jnp.float32),
        derivative_of_multiple.astype(jnp.float32) * shorts[1].astype(jnp.float32)]).astype(jnp.bfloat16)
    gradients = anticausal_taps(grad_shorts, short_weights).astype(jnp.bfloat16)
    return mixed_out, gradients[0], gradients[1], gradients[2], grad_filters, grad_out_weight
```

```python
import math

import jax
import jax.numpy as jnp
from jax import lax
from jax.sharding import PartitionSpec as P

BLOCK = 128


TWO_PI = 2.0 * math.pi
HIGHEST = lax.Precision.HIGHEST


def from_behind(value, axis, steps):
    count = lax.axis_size(axis)
    first, last = (max(0, -steps), min(count, count - steps))
    return lax.ppermute(value, axis, [(source, source + steps) for source in range(first, last)])


def fourier_table(count):
    element_indices = jnp.arange(count, dtype=jnp.int32)
    angles = (element_indices[:, None] * element_indices[None, :] % count).astype(jnp.float32) * (
        TWO_PI / count
    )
    return (jnp.cos(angles), -jnp.sin(angles))


def make_tables(length, block_width):
    row_count = 2 * length // block_width
    full_len = row_count * block_width
    outer_re, outer_im = fourier_table(row_count)
    inner_re, inner_im = fourier_table(block_width)
    row_index = jnp.arange(row_count, dtype=jnp.int32)[:, None]
    col_index = jnp.arange(block_width, dtype=jnp.int32)[None, :]
    angles = (row_index * col_index % full_len).astype(jnp.float32) * (TWO_PI / full_len)
    return (outer_re, outer_im, inner_re, inner_im, jnp.cos(angles), -jnp.sin(angles))


def spectrum(signal, tables):
    outer_re, outer_im, inner_re, inner_im, twist_re, twist_im = tables
    channels, length = signal.shape
    block_width = inner_re.shape[0]
    half_rows = length // block_width
    blocks = signal.reshape(channels, half_rows, block_width)
    section_re = jnp.einsum("kn,cnm->ckm", outer_re[:, :half_rows], blocks, precision=HIGHEST)
    section_im = jnp.einsum("kn,cnm->ckm", outer_im[:, :half_rows], blocks, precision=HIGHEST)
    turned_re = section_re * twist_re - section_im * twist_im
    turned_im = section_re * twist_im + section_im * twist_re
    frequency_real_component = jnp.matmul(turned_re, inner_re, precision=HIGHEST) - jnp.matmul(
        turned_im, inner_im, precision=HIGHEST
    )
    spec_im = jnp.matmul(turned_re, inner_im, precision=HIGHEST) + jnp.matmul(
        turned_im, inner_re, precision=HIGHEST
    )
    return (frequency_real_component, spec_im)


def inverse(frequency_real_component, spec_im, tables):
    outer_re, outer_im, inner_re, inner_im, twist_re, twist_im = tables
    channels, row_count, block_width = frequency_real_component.shape
    half_rows = row_count // 2
    back_re = jnp.matmul(frequency_real_component, inner_re, precision=HIGHEST) + jnp.matmul(
        spec_im, inner_im, precision=HIGHEST
    )
    back_im = jnp.matmul(spec_im, inner_re, precision=HIGHEST) - jnp.matmul(
        frequency_real_component, inner_im, precision=HIGHEST
    )
    turned_re = back_re * twist_re + back_im * twist_im
    turned_im = back_im * twist_re - back_re * twist_im
    signal = jnp.einsum("nk,ckm->cnm", outer_re[:half_rows], turned_re, precision=HIGHEST)
    signal = signal + jnp.einsum("nk,ckm->cnm", outer_im[:half_rows], turned_im, precision=HIGHEST)
    return (signal / (row_count * block_width)).reshape(channels, half_rows * block_width)


def causal_taps(stacked, earlier, weights):
    tap_count = weights.shape[2]
    length = stacked.shape[2]
    extended = jnp.concatenate([earlier, stacked], axis=2).astype(jnp.float32)
    running_total = jnp.zeros(stacked.shape, jnp.float32)
    for offset in range(tap_count):
        begin = tap_count - 1 - offset
        running_total = (
            running_total
            + weights[:, :, offset : offset + 1] * extended[:, :, begin : begin + length]
        )
    return running_total


def anticausal_taps(stacked, following, weights):
    tap_count = weights.shape[2]
    length = stacked.shape[2]
    extended = jnp.concatenate([stacked, following], axis=2).astype(jnp.float32)
    running_total = jnp.zeros(stacked.shape, jnp.float32)
    for offset in range(tap_count):
        running_total = (
            running_total
            + weights[:, :, offset : offset + 1] * extended[:, :, offset : offset + length]
        )
    return running_total


def to_channels(block):
    return lax.all_to_all(block, "ctx", split_axis=0, concat_axis=1, tiled=True)


def to_positions(block):
    return lax.all_to_all(block, "ctx", split_axis=1, concat_axis=0, tiled=True)


def per_device(query_in, key_in, value_in, short_weights, filters, out_weight, cotangent):
    tap_count = short_weights.shape[2]
    local_len = query_in.shape[1]
    stacked = jnp.stack([query_in, key_in, value_in])
    earlier = from_behind(stacked[:, :, local_len - (tap_count - 1) :], "ctx", 1)
    shorts = causal_taps(stacked, earlier, short_weights).astype(jnp.bfloat16)
    product = (shorts[1].astype(jnp.float32) * shorts[2].astype(jnp.float32)).astype(jnp.bfloat16)
    product_chan = to_channels(product)
    tables = make_tables(product_chan.shape[1], BLOCK)
    kernel_re, kernel_im = spectrum(filters[0], tables)
    product_re, product_im = spectrum(product_chan.astype(jnp.float32), tables)
    convolved_chan = inverse(
        product_re * kernel_re - product_im * kernel_im,
        product_re * kernel_im + product_im * kernel_re,
        tables,
    ).astype(jnp.bfloat16)
    convolved = to_positions(convolved_chan)
    gated_out = (shorts[0].astype(jnp.float32) * convolved.astype(jnp.float32)).astype(jnp.bfloat16)
    mixed_out = lax.psum_scatter(
        jnp.dot(out_weight, gated_out, preferred_element_type=jnp.float32).astype(jnp.bfloat16),
        "tp",
        scatter_dimension=0,
        tiled=True,
    )
    full_cotangent = lax.all_gather(cotangent, "tp", axis=0, tiled=True)
    grad_gated = lax.dot_general(
        out_weight, full_cotangent, (((0,), (0,)), ((), ())), preferred_element_type=jnp.float32
    )
    ctx_count = lax.axis_size("ctx")
    weight_partial = lax.dot_general(
        full_cotangent, gated_out, (((1,), (1,)), ((), ())), preferred_element_type=jnp.float32
    ).astype(jnp.bfloat16)
    weight_partial = weight_partial.reshape(ctx_count, -1, weight_partial.shape[1])
    grad_out_weight = lax.all_to_all(
        weight_partial, "ctx", split_axis=0, concat_axis=0, tiled=True
    ).astype(jnp.float32).sum(0)
    grad_conv = (grad_gated * shorts[0].astype(jnp.float32)).astype(jnp.bfloat16)
    grad_chan = to_channels(grad_conv)
    gradient_re, gradient_im = spectrum(grad_chan.astype(jnp.float32), tables)
    grad_product_chan = inverse(
        kernel_re * gradient_re + kernel_im * gradient_im,
        kernel_re * gradient_im - kernel_im * gradient_re,
        tables,
    ).astype(jnp.bfloat16)
    grad_filters = inverse(
        product_re * gradient_re + product_im * gradient_im,
        product_re * gradient_im - product_im * gradient_re,
        tables,
    ).reshape(filters.shape)
    derivative_of_multiple = to_positions(grad_product_chan)
    grad_shorts = jnp.stack(
        [
            grad_gated * convolved.astype(jnp.float32),
            derivative_of_multiple.astype(jnp.float32) * shorts[2].astype(jnp.float32),
            derivative_of_multiple.astype(jnp.float32) * shorts[1].astype(jnp.float32),
        ]
    ).astype(jnp.bfloat16)
    following = from_behind(grad_shorts[:, :, : tap_count - 1], "ctx", -1)
    gradients = anticausal_taps(grad_shorts, following, short_weights).astype(jnp.bfloat16)
    return (mixed_out, gradients[0], gradients[1], gradients[2], grad_filters, grad_out_weight)


def solution(mesh):
    placed = (
        P("tp", "ctx"),
        P("tp", "ctx"),
        P("tp", "ctx"),
        P(None, "tp", None),
        P("tp", "ctx", None),
        P(None, "tp"),
        P("tp", "ctx"),
    )
    return jax.shard_map(
        per_device,
        mesh=mesh,
        in_specs=placed,
        out_specs=(
            P("tp", "ctx"),
            P("tp", "ctx"),
            P("tp", "ctx"),
            P("tp", "ctx"),
            P("tp", "ctx", None),
            P("ctx", "tp"),
        ),
        check_vma=False,
    )
```

```python
import math

import jax
import jax.numpy as jnp
from jax import lax
from jax.sharding import Mesh, PartitionSpec as P

BLOCK = 128
CTX_HI = "ctx_hi"
CTX_LO = "ctx_lo"
CTX = (CTX_HI, CTX_LO)
LO_SIZE = 8


TWO_PI = 2.0 * math.pi
HIGHEST = lax.Precision.HIGHEST


def from_behind(value, axis, steps):
    count = lax.axis_size(axis)
    first, last = (max(0, -steps), min(count, count - steps))
    return lax.ppermute(value, axis, [(source, source + steps) for source in range(first, last)])


def fourier_table(count):
    element_indices = jnp.arange(count, dtype=jnp.int32)
    angles = (element_indices[:, None] * element_indices[None, :] % count).astype(jnp.float32) * (
        TWO_PI / count
    )
    return (jnp.cos(angles), -jnp.sin(angles))


def make_tables(length, block_width):
    row_count = 2 * length // block_width
    full_len = row_count * block_width
    outer_re, outer_im = fourier_table(row_count)
    inner_re, inner_im = fourier_table(block_width)
    row_index = jnp.arange(row_count, dtype=jnp.int32)[:, None]
    col_index = jnp.arange(block_width, dtype=jnp.int32)[None, :]
    angles = (row_index * col_index % full_len).astype(jnp.float32) * (TWO_PI / full_len)
    return (outer_re, outer_im, inner_re, inner_im, jnp.cos(angles), -jnp.sin(angles))


def spectrum(signal, tables):
    outer_re, outer_im, inner_re, inner_im, twist_re, twist_im = tables
    channels, length = signal.shape
    block_width = inner_re.shape[0]
    half_rows = length // block_width
    blocks = signal.reshape(channels, half_rows, block_width)
    section_re = jnp.einsum("kn,cnm->ckm", outer_re[:, :half_rows], blocks, precision=HIGHEST)
    section_im = jnp.einsum("kn,cnm->ckm", outer_im[:, :half_rows], blocks, precision=HIGHEST)
    turned_re = section_re * twist_re - section_im * twist_im
    turned_im = section_re * twist_im + section_im * twist_re
    frequency_real_component = jnp.matmul(turned_re, inner_re, precision=HIGHEST) - jnp.matmul(
        turned_im, inner_im, precision=HIGHEST
    )
    spec_im = jnp.matmul(turned_re, inner_im, precision=HIGHEST) + jnp.matmul(
        turned_im, inner_re, precision=HIGHEST
    )
    return (frequency_real_component, spec_im)


def inverse(frequency_real_component, spec_im, tables):
    outer_re, outer_im, inner_re, inner_im, twist_re, twist_im = tables
    channels, row_count, block_width = frequency_real_component.shape
    half_rows = row_count // 2
    back_re = jnp.matmul(frequency_real_component, inner_re, precision=HIGHEST) + jnp.matmul(
        spec_im, inner_im, precision=HIGHEST
    )
    back_im = jnp.matmul(spec_im, inner_re, precision=HIGHEST) - jnp.matmul(
        frequency_real_component, inner_im, precision=HIGHEST
    )
    turned_re = back_re * twist_re + back_im * twist_im
    turned_im = back_im * twist_re - back_re * twist_im
    signal = jnp.einsum("nk,ckm->cnm", outer_re[:half_rows], turned_re, precision=HIGHEST)
    signal = signal + jnp.einsum("nk,ckm->cnm", outer_im[:half_rows], turned_im, precision=HIGHEST)
    return (signal / (row_count * block_width)).reshape(channels, half_rows * block_width)


def causal_taps(stacked, earlier, weights):
    tap_count = weights.shape[2]
    length = stacked.shape[2]
    extended = jnp.concatenate([earlier, stacked], axis=2).astype(jnp.float32)
    running_total = jnp.zeros(stacked.shape, jnp.float32)
    for offset in range(tap_count):
        begin = tap_count - 1 - offset
        running_total = (
            running_total
            + weights[:, :, offset : offset + 1] * extended[:, :, begin : begin + length]
        )
    return running_total


def anticausal_taps(stacked, following, weights):
    tap_count = weights.shape[2]
    length = stacked.shape[2]
    extended = jnp.concatenate([stacked, following], axis=2).astype(jnp.float32)
    running_total = jnp.zeros(stacked.shape, jnp.float32)
    for offset in range(tap_count):
        running_total = (
            running_total
            + weights[:, :, offset : offset + 1] * extended[:, :, offset : offset + length]
        )
    return running_total


def to_channels(block):
    return lax.all_to_all(block, CTX, split_axis=0, concat_axis=1, tiled=True)


def to_positions(block):
    return lax.all_to_all(block, CTX, split_axis=1, concat_axis=0, tiled=True)


def weight_gradient(full_cotangent, gated_out):
    hi_count = lax.axis_size(CTX_HI)
    lo_count = lax.axis_size(CTX_LO)
    features, local_len = full_cotangent.shape
    rows = features // (hi_count * lo_count)
    group_gated = lax.all_gather(gated_out, CTX_LO, axis=1, tiled=True)
    group_gated = group_gated.reshape(gated_out.shape[0], lo_count, local_len)
    by_target = full_cotangent.reshape(hi_count, lo_count, rows, local_len).transpose(1, 0, 2, 3)
    group_rows = lax.all_to_all(by_target, CTX_LO, split_axis=0, concat_axis=0, tiled=True)
    weight_partial = lax.dot_general(
        group_rows, group_gated, (((0, 3), (1, 2)), ((), ())), preferred_element_type=jnp.float32
    ).astype(jnp.bfloat16)
    received = lax.all_to_all(weight_partial, CTX_HI, split_axis=0, concat_axis=0, tiled=True)
    return received.astype(jnp.float32).sum(0)


def per_device(query_in, key_in, value_in, short_weights, filters, out_weight, cotangent):
    tap_count = short_weights.shape[2]
    local_len = query_in.shape[1]
    stacked = jnp.stack([query_in, key_in, value_in])
    earlier = from_behind(stacked[:, :, local_len - (tap_count - 1) :], CTX, 1)
    shorts = causal_taps(stacked, earlier, short_weights).astype(jnp.bfloat16)
    product = (shorts[1].astype(jnp.float32) * shorts[2].astype(jnp.float32)).astype(jnp.bfloat16)
    product_chan = to_channels(product)
    tables = make_tables(product_chan.shape[1], BLOCK)
    kernel_re, kernel_im = spectrum(filters[0], tables)
    product_re, product_im = spectrum(product_chan.astype(jnp.float32), tables)
    convolved_chan = inverse(
        product_re * kernel_re - product_im * kernel_im,
        product_re * kernel_im + product_im * kernel_re,
        tables,
    ).astype(jnp.bfloat16)
    convolved = to_positions(convolved_chan)
    gated_out = (shorts[0].astype(jnp.float32) * convolved.astype(jnp.float32)).astype(jnp.bfloat16)
    mixed_out = lax.psum_scatter(
        jnp.dot(out_weight, gated_out, preferred_element_type=jnp.float32).astype(jnp.bfloat16),
        "tp",
        scatter_dimension=0,
        tiled=True,
    )
    full_cotangent = lax.all_gather(cotangent, "tp", axis=0, tiled=True)
    grad_gated = lax.dot_general(
        out_weight, full_cotangent, (((0,), (0,)), ((), ())), preferred_element_type=jnp.float32
    )
    grad_out_weight = weight_gradient(full_cotangent, gated_out)
    grad_conv = (grad_gated * shorts[0].astype(jnp.float32)).astype(jnp.bfloat16)
    grad_chan = to_channels(grad_conv)
    gradient_re, gradient_im = spectrum(grad_chan.astype(jnp.float32), tables)
    grad_product_chan = inverse(
        kernel_re * gradient_re + kernel_im * gradient_im,
        kernel_re * gradient_im - kernel_im * gradient_re,
        tables,
    ).astype(jnp.bfloat16)
    grad_filters = inverse(
        product_re * gradient_re + product_im * gradient_im,
        product_re * gradient_im - product_im * gradient_re,
        tables,
    ).reshape(filters.shape)
    derivative_of_multiple = to_positions(grad_product_chan)
    grad_shorts = jnp.stack(
        [
            grad_gated * convolved.astype(jnp.float32),
            derivative_of_multiple.astype(jnp.float32) * shorts[2].astype(jnp.float32),
            derivative_of_multiple.astype(jnp.float32) * shorts[1].astype(jnp.float32),
        ]
    ).astype(jnp.bfloat16)
    following = from_behind(grad_shorts[:, :, : tap_count - 1], CTX, -1)
    gradients = anticausal_taps(grad_shorts, following, short_weights).astype(jnp.bfloat16)
    return (mixed_out, gradients[0], gradients[1], gradients[2], grad_filters, grad_out_weight)


def solution(mesh):
    ctx_count, tp_count = mesh.devices.shape
    split_mesh = Mesh(
        mesh.devices.reshape(ctx_count // LO_SIZE, LO_SIZE, tp_count), (CTX_HI, CTX_LO, "tp")
    )
    placed = (
        P("tp", CTX),
        P("tp", CTX),
        P("tp", CTX),
        P(None, "tp", None),
        P("tp", CTX, None),
        P(None, "tp"),
        P("tp", CTX),
    )
    return jax.shard_map(
        per_device,
        mesh=split_mesh,
        in_specs=placed,
        out_specs=(
            P("tp", CTX),
            P("tp", CTX),
            P("tp", CTX),
            P("tp", CTX),
            P("tp", CTX, None),
            P(CTX, "tp"),
        ),
        check_vma=False,
    )
```

```python
import math

import jax
import jax.numpy as jnp
from jax import lax
from jax.sharding import Mesh, PartitionSpec as P

BLOCK = 128
CTX_HI = "ctx_hi"
CTX_LO = "ctx_lo"
CTX = (CTX_HI, CTX_LO)
LO_SIZE = 8


TWO_PI = 2.0 * math.pi
HIGHEST = lax.Precision.HIGHEST


def from_behind(value, axis, steps):
    count = lax.axis_size(axis)
    first, last = (max(0, -steps), min(count, count - steps))
    return lax.ppermute(value, axis, [(source, source + steps) for source in range(first, last)])


def fourier_table(count):
    element_indices = jnp.arange(count, dtype=jnp.int32)
    angles = (element_indices[:, None] * element_indices[None, :] % count).astype(jnp.float32) * (
        TWO_PI / count
    )
    return (jnp.cos(angles), -jnp.sin(angles))


def make_tables(length, block_width):
    row_count = 2 * length // block_width
    full_len = row_count * block_width
    outer_re, outer_im = fourier_table(row_count)
    inner_re, inner_im = fourier_table(block_width)
    row_index = jnp.arange(row_count, dtype=jnp.int32)[:, None]
    col_index = jnp.arange(block_width, dtype=jnp.int32)[None, :]
    angles = (row_index * col_index % full_len).astype(jnp.float32) * (TWO_PI / full_len)
    return (outer_re, outer_im, inner_re, inner_im, jnp.cos(angles), -jnp.sin(angles))


def spectrum(signal, tables):
    outer_re, outer_im, inner_re, inner_im, twist_re, twist_im = tables
    channels, length = signal.shape
    block_width = inner_re.shape[0]
    half_rows = length // block_width
    blocks = signal.reshape(channels, half_rows, block_width)
    section_re = jnp.einsum("kn,cnm->ckm", outer_re[:, :half_rows], blocks, precision=HIGHEST)
    section_im = jnp.einsum("kn,cnm->ckm", outer_im[:, :half_rows], blocks, precision=HIGHEST)
    turned_re = section_re * twist_re - section_im * twist_im
    turned_im = section_re * twist_im + section_im * twist_re
    frequency_real_component = jnp.matmul(turned_re, inner_re, precision=HIGHEST) - jnp.matmul(
        turned_im, inner_im, precision=HIGHEST
    )
    spec_im = jnp.matmul(turned_re, inner_im, precision=HIGHEST) + jnp.matmul(
        turned_im, inner_re, precision=HIGHEST
    )
    return (frequency_real_component, spec_im)


def inverse(frequency_real_component, spec_im, tables):
    outer_re, outer_im, inner_re, inner_im, twist_re, twist_im = tables
    channels, row_count, block_width = frequency_real_component.shape
    half_rows = row_count // 2
    back_re = jnp.matmul(frequency_real_component, inner_re, precision=HIGHEST) + jnp.matmul(
        spec_im, inner_im, precision=HIGHEST
    )
    back_im = jnp.matmul(spec_im, inner_re, precision=HIGHEST) - jnp.matmul(
        frequency_real_component, inner_im, precision=HIGHEST
    )
    turned_re = back_re * twist_re + back_im * twist_im
    turned_im = back_im * twist_re - back_re * twist_im
    signal = jnp.einsum("nk,ckm->cnm", outer_re[:half_rows], turned_re, precision=HIGHEST)
    signal = signal + jnp.einsum("nk,ckm->cnm", outer_im[:half_rows], turned_im, precision=HIGHEST)
    return (signal / (row_count * block_width)).reshape(channels, half_rows * block_width)


def causal_taps(stacked, earlier, weights):
    tap_count = weights.shape[2]
    length = stacked.shape[2]
    extended = jnp.concatenate([earlier, stacked], axis=2).astype(jnp.float32)
    running_total = jnp.zeros(stacked.shape, jnp.float32)
    for offset in range(tap_count):
        begin = tap_count - 1 - offset
        running_total = (
            running_total
            + weights[:, :, offset : offset + 1] * extended[:, :, begin : begin + length]
        )
    return running_total


def anticausal_taps(stacked, following, weights):
    tap_count = weights.shape[2]
    length = stacked.shape[2]
    extended = jnp.concatenate([stacked, following], axis=2).astype(jnp.float32)
    running_total = jnp.zeros(stacked.shape, jnp.float32)
    for offset in range(tap_count):
        running_total = (
            running_total
            + weights[:, :, offset : offset + 1] * extended[:, :, offset : offset + length]
        )
    return running_total


def to_channels(block):
    return lax.all_to_all(block, CTX, split_axis=0, concat_axis=1, tiled=True)


def to_positions(block):
    return lax.all_to_all(block, CTX, split_axis=1, concat_axis=0, tiled=True)


def weight_gradient(full_cotangent, gated_out):
    hi_count = lax.axis_size(CTX_HI)
    lo_count = lax.axis_size(CTX_LO)
    features, local_len = full_cotangent.shape
    rows = features // (hi_count * lo_count)
    group_gated = lax.all_gather(gated_out, CTX_LO, axis=1, tiled=True)
    group_gated = group_gated.reshape(gated_out.shape[0], lo_count, local_len)
    by_target = full_cotangent.reshape(hi_count, lo_count, rows, local_len).transpose(1, 0, 2, 3)
    group_rows = lax.all_to_all(by_target, CTX_LO, split_axis=0, concat_axis=0, tiled=True)
    weight_partial = lax.dot_general(
        group_rows, group_gated, (((0, 3), (1, 2)), ((), ())), preferred_element_type=jnp.float32
    ).astype(jnp.bfloat16)
    received = lax.all_to_all(weight_partial, CTX_HI, split_axis=0, concat_axis=0, tiled=True)
    return received.astype(jnp.float32).sum(0)


def per_device(query_in, key_in, value_in, short_weights, filters, out_weight, cotangent):
    tap_count = short_weights.shape[2]
    local_len = query_in.shape[1]
    stacked = jnp.stack([query_in, key_in, value_in])
    earlier = from_behind(stacked[:, :, local_len - (tap_count - 1) :], CTX, 1)
    shorts = causal_taps(stacked, earlier, short_weights).astype(jnp.bfloat16)
    product = (shorts[1].astype(jnp.float32) * shorts[2].astype(jnp.float32)).astype(jnp.bfloat16)
    full_cotangent = lax.all_gather(cotangent, "tp", axis=0, tiled=True)
    grad_gated = lax.dot_general(
        out_weight, full_cotangent, (((0,), (0,)), ((), ())), preferred_element_type=jnp.float32
    )
    grad_conv = (grad_gated * shorts[0].astype(jnp.float32)).astype(jnp.bfloat16)
    channels = product.shape[0] // lax.axis_size(CTX)
    both_chan = lax.all_to_all(
        jnp.stack([product, grad_conv]), CTX, split_axis=1, concat_axis=2, tiled=True
    )
    tables = make_tables(both_chan.shape[2], BLOCK)
    kernel_re, kernel_im = spectrum(filters[0], tables)
    both_re, both_im = spectrum(
        both_chan.reshape(2 * channels, -1).astype(jnp.float32), tables
    )
    product_re, gradient_re = both_re[:channels], both_re[channels:]
    product_im, gradient_im = both_im[:channels], both_im[channels:]
    three_re = jnp.concatenate(
        [
            product_re * kernel_re - product_im * kernel_im,
            kernel_re * gradient_re + kernel_im * gradient_im,
            product_re * gradient_re + product_im * gradient_im,
        ]
    )
    three_im = jnp.concatenate(
        [
            product_re * kernel_im + product_im * kernel_re,
            kernel_re * gradient_im - kernel_im * gradient_re,
            product_re * gradient_im - product_im * gradient_re,
        ]
    )
    three = inverse(three_re, three_im, tables)
    grad_filters = three[2 * channels :].reshape(filters.shape)
    back_chan = three[: 2 * channels].astype(jnp.bfloat16).reshape(2, channels, -1)
    back = lax.all_to_all(back_chan, CTX, split_axis=2, concat_axis=1, tiled=True)
    convolved, derivative_of_multiple = back[0], back[1]
    gated_out = (shorts[0].astype(jnp.float32) * convolved.astype(jnp.float32)).astype(jnp.bfloat16)
    mixed_out = lax.psum_scatter(
        jnp.dot(out_weight, gated_out, preferred_element_type=jnp.float32).astype(jnp.bfloat16),
        "tp",
        scatter_dimension=0,
        tiled=True,
    )
    grad_out_weight = weight_gradient(full_cotangent, gated_out)
    grad_shorts = jnp.stack(
        [
            grad_gated * convolved.astype(jnp.float32),
            derivative_of_multiple.astype(jnp.float32) * shorts[2].astype(jnp.float32),
            derivative_of_multiple.astype(jnp.float32) * shorts[1].astype(jnp.float32),
        ]
    ).astype(jnp.bfloat16)
    following = from_behind(grad_shorts[:, :, : tap_count - 1], CTX, -1)
    gradients = anticausal_taps(grad_shorts, following, short_weights).astype(jnp.bfloat16)
    return (mixed_out, gradients[0], gradients[1], gradients[2], grad_filters, grad_out_weight)


def solution(mesh):
    ctx_count, tp_count = mesh.devices.shape
    split_mesh = Mesh(
        mesh.devices.reshape(ctx_count // LO_SIZE, LO_SIZE, tp_count), (CTX_HI, CTX_LO, "tp")
    )
    placed = (
        P("tp", CTX),
        P("tp", CTX),
        P("tp", CTX),
        P(None, "tp", None),
        P("tp", CTX, None),
        P(None, "tp"),
        P("tp", CTX),
    )
    return jax.shard_map(
        per_device,
        mesh=split_mesh,
        in_specs=placed,
        out_specs=(
            P("tp", CTX),
            P("tp", CTX),
            P("tp", CTX),
            P("tp", CTX),
            P("tp", CTX, None),
            P(CTX, "tp"),
        ),
        check_vma=False,
    )
```

```python
import math

import jax
import jax.numpy as jnp
from jax import lax
from jax.sharding import Mesh, PartitionSpec as P

BLOCK = 128
CTX_HI = "ctx_hi"
CTX_LO = "ctx_lo"
CTX = (CTX_HI, CTX_LO)
LO_SIZE = 8


TWO_PI = 2.0 * math.pi
HIGHEST = lax.Precision.HIGHEST


def from_behind(value, axis, steps):
    count = lax.axis_size(axis)
    first, last = (max(0, -steps), min(count, count - steps))
    return lax.ppermute(value, axis, [(source, source + steps) for source in range(first, last)])


def fourier_table(count):
    element_indices = jnp.arange(count, dtype=jnp.int32)
    angles = (element_indices[:, None] * element_indices[None, :] % count).astype(jnp.float32) * (
        TWO_PI / count
    )
    return (jnp.cos(angles), -jnp.sin(angles))


def make_tables(length, block_width):
    row_count = 2 * length // block_width
    full_len = row_count * block_width
    outer_re, outer_im = fourier_table(row_count)
    inner_re, inner_im = fourier_table(block_width)
    row_index = jnp.arange(row_count, dtype=jnp.int32)[:, None]
    col_index = jnp.arange(block_width, dtype=jnp.int32)[None, :]
    angles = (row_index * col_index % full_len).astype(jnp.float32) * (TWO_PI / full_len)
    return (outer_re, outer_im, inner_re, inner_im, jnp.cos(angles), -jnp.sin(angles))


def spectrum(signal, tables):
    outer_re, outer_im, inner_re, inner_im, twist_re, twist_im = tables
    channels, length = signal.shape
    block_width = inner_re.shape[0]
    half_rows = length // block_width
    blocks = signal.reshape(channels, half_rows, block_width)
    section_re = jnp.einsum("kn,cnm->ckm", outer_re[:, :half_rows], blocks, precision=HIGHEST)
    section_im = jnp.einsum("kn,cnm->ckm", outer_im[:, :half_rows], blocks, precision=HIGHEST)
    turned_re = section_re * twist_re - section_im * twist_im
    turned_im = section_re * twist_im + section_im * twist_re
    frequency_real_component = jnp.matmul(turned_re, inner_re, precision=HIGHEST) - jnp.matmul(
        turned_im, inner_im, precision=HIGHEST
    )
    spec_im = jnp.matmul(turned_re, inner_im, precision=HIGHEST) + jnp.matmul(
        turned_im, inner_re, precision=HIGHEST
    )
    return (frequency_real_component, spec_im)


def inverse(frequency_real_component, spec_im, tables):
    outer_re, outer_im, inner_re, inner_im, twist_re, twist_im = tables
    channels, row_count, block_width = frequency_real_component.shape
    half_rows = row_count // 2
    back_re = jnp.matmul(frequency_real_component, inner_re, precision=HIGHEST) + jnp.matmul(
        spec_im, inner_im, precision=HIGHEST
    )
    back_im = jnp.matmul(spec_im, inner_re, precision=HIGHEST) - jnp.matmul(
        frequency_real_component, inner_im, precision=HIGHEST
    )
    turned_re = back_re * twist_re + back_im * twist_im
    turned_im = back_im * twist_re - back_re * twist_im
    signal = jnp.einsum("nk,ckm->cnm", outer_re[:half_rows], turned_re, precision=HIGHEST)
    signal = signal + jnp.einsum("nk,ckm->cnm", outer_im[:half_rows], turned_im, precision=HIGHEST)
    return (signal / (row_count * block_width)).reshape(channels, half_rows * block_width)


def causal_taps(stacked, earlier, weights):
    tap_count = weights.shape[2]
    length = stacked.shape[2]
    extended = jnp.concatenate([earlier, stacked], axis=2).astype(jnp.float32)
    running_total = jnp.zeros(stacked.shape, jnp.float32)
    for offset in range(tap_count):
        begin = tap_count - 1 - offset
        running_total = (
            running_total
            + weights[:, :, offset : offset + 1] * extended[:, :, begin : begin + length]
        )
    return running_total


def anticausal_taps(stacked, following, weights):
    tap_count = weights.shape[2]
    length = stacked.shape[2]
    extended = jnp.concatenate([stacked, following], axis=2).astype(jnp.float32)
    running_total = jnp.zeros(stacked.shape, jnp.float32)
    for offset in range(tap_count):
        running_total = (
            running_total
            + weights[:, :, offset : offset + 1] * extended[:, :, offset : offset + length]
        )
    return running_total


def to_channels(block):
    return lax.all_to_all(block, CTX, split_axis=0, concat_axis=1, tiled=True)


def to_positions(block):
    return lax.all_to_all(block, CTX, split_axis=1, concat_axis=0, tiled=True)


def swap_layouts(channel_block, position_block):
    count = lax.axis_size(CTX)
    channels, length = channel_block.shape
    local_len = length // count
    outgoing = jnp.stack(
        [
            channel_block.reshape(channels, count, local_len).transpose(1, 0, 2),
            position_block.reshape(count, channels, local_len),
        ],
        axis=1,
    )
    incoming = lax.all_to_all(outgoing, CTX, split_axis=0, concat_axis=0, tiled=True)
    positions = incoming[:, 0].reshape(count * channels, local_len)
    channels_out = incoming[:, 1].transpose(1, 0, 2).reshape(channels, length)
    return positions, channels_out


def weight_gradient(full_cotangent, gated_out):
    hi_count = lax.axis_size(CTX_HI)
    lo_count = lax.axis_size(CTX_LO)
    features, local_len = full_cotangent.shape
    rows = features // (hi_count * lo_count)
    group_gated = lax.all_gather(gated_out, CTX_LO, axis=1, tiled=True)
    group_gated = group_gated.reshape(gated_out.shape[0], lo_count, local_len)
    by_target = full_cotangent.reshape(hi_count, lo_count, rows, local_len).transpose(1, 0, 2, 3)
    group_rows = lax.all_to_all(by_target, CTX_LO, split_axis=0, concat_axis=0, tiled=True)
    weight_partial = lax.dot_general(
        group_rows, group_gated, (((0, 3), (1, 2)), ((), ())), preferred_element_type=jnp.float32
    ).astype(jnp.bfloat16)
    received = lax.all_to_all(weight_partial, CTX_HI, split_axis=0, concat_axis=0, tiled=True)
    return received.astype(jnp.float32).sum(0)


def per_device(query_in, key_in, value_in, short_weights, filters, out_weight, cotangent):
    tap_count = short_weights.shape[2]
    local_len = query_in.shape[1]
    stacked = jnp.stack([query_in, key_in, value_in])
    earlier = from_behind(stacked[:, :, local_len - (tap_count - 1) :], CTX, 1)
    shorts = causal_taps(stacked, earlier, short_weights).astype(jnp.bfloat16)
    product = (shorts[1].astype(jnp.float32) * shorts[2].astype(jnp.float32)).astype(jnp.bfloat16)
    product_chan = to_channels(product)
    tables = make_tables(product_chan.shape[1], BLOCK)
    kernel_re, kernel_im = spectrum(filters[0], tables)
    product_re, product_im = spectrum(product_chan.astype(jnp.float32), tables)
    convolved_chan = inverse(
        product_re * kernel_re - product_im * kernel_im,
        product_re * kernel_im + product_im * kernel_re,
        tables,
    ).astype(jnp.bfloat16)
    full_cotangent = lax.all_gather(cotangent, "tp", axis=0, tiled=True)
    grad_gated = lax.dot_general(
        out_weight, full_cotangent, (((0,), (0,)), ((), ())), preferred_element_type=jnp.float32
    )
    grad_conv = (grad_gated * shorts[0].astype(jnp.float32)).astype(jnp.bfloat16)
    convolved, grad_chan = swap_layouts(convolved_chan, grad_conv)
    gated_out = (shorts[0].astype(jnp.float32) * convolved.astype(jnp.float32)).astype(jnp.bfloat16)
    mixed_out = lax.psum_scatter(
        jnp.dot(out_weight, gated_out, preferred_element_type=jnp.float32).astype(jnp.bfloat16),
        "tp",
        scatter_dimension=0,
        tiled=True,
    )
    grad_out_weight = weight_gradient(full_cotangent, gated_out)
    gradient_re, gradient_im = spectrum(grad_chan.astype(jnp.float32), tables)
    grad_product_chan = inverse(
        kernel_re * gradient_re + kernel_im * gradient_im,
        kernel_re * gradient_im - kernel_im * gradient_re,
        tables,
    ).astype(jnp.bfloat16)
    grad_filters = inverse(
        product_re * gradient_re + product_im * gradient_im,
        product_re * gradient_im - product_im * gradient_re,
        tables,
    ).reshape(filters.shape)
    derivative_of_multiple = to_positions(grad_product_chan)
    grad_shorts = jnp.stack(
        [
            grad_gated * convolved.astype(jnp.float32),
            derivative_of_multiple.astype(jnp.float32) * shorts[2].astype(jnp.float32),
            derivative_of_multiple.astype(jnp.float32) * shorts[1].astype(jnp.float32),
        ]
    ).astype(jnp.bfloat16)
    following = from_behind(grad_shorts[:, :, : tap_count - 1], CTX, -1)
    gradients = anticausal_taps(grad_shorts, following, short_weights).astype(jnp.bfloat16)
    return (mixed_out, gradients[0], gradients[1], gradients[2], grad_filters, grad_out_weight)


def solution(mesh):
    ctx_count, tp_count = mesh.devices.shape
    split_mesh = Mesh(
        mesh.devices.reshape(ctx_count // LO_SIZE, LO_SIZE, tp_count), (CTX_HI, CTX_LO, "tp")
    )
    placed = (
        P("tp", CTX),
        P("tp", CTX),
        P("tp", CTX),
        P(None, "tp", None),
        P("tp", CTX, None),
        P(None, "tp"),
        P("tp", CTX),
    )
    return jax.shard_map(
        per_device,
        mesh=split_mesh,
        in_specs=placed,
        out_specs=(
            P("tp", CTX),
            P("tp", CTX),
            P("tp", CTX),
            P("tp", CTX),
            P("tp", CTX, None),
            P(CTX, "tp"),
        ),
        check_vma=False,
    )
```

```python
import math

import jax
import jax.numpy as jnp
from jax import lax
from jax.sharding import Mesh, PartitionSpec as P

BLOCK = 128
CTX_HI = "ctx_hi"
CTX_LO = "ctx_lo"
CTX = (CTX_HI, CTX_LO)
LO_SIZE = 8


TWO_PI = 2.0 * math.pi
HIGHEST = lax.Precision.HIGHEST


def from_behind(value, axis, steps):
    count = lax.axis_size(axis)
    first, last = (max(0, -steps), min(count, count - steps))
    return lax.ppermute(value, axis, [(source, source + steps) for source in range(first, last)])


def fourier_table(count):
    element_indices = jnp.arange(count, dtype=jnp.int32)
    angles = (element_indices[:, None] * element_indices[None, :] % count).astype(jnp.float32) * (
        TWO_PI / count
    )
    return (jnp.cos(angles), -jnp.sin(angles))


def make_tables(length, block_width):
    row_count = 2 * length // block_width
    full_len = row_count * block_width
    outer_re, outer_im = fourier_table(row_count)
    inner_re, inner_im = fourier_table(block_width)
    row_index = jnp.arange(row_count, dtype=jnp.int32)[:, None]
    col_index = jnp.arange(block_width, dtype=jnp.int32)[None, :]
    angles = (row_index * col_index % full_len).astype(jnp.float32) * (TWO_PI / full_len)
    return (outer_re, outer_im, inner_re, inner_im, jnp.cos(angles), -jnp.sin(angles))


def spectrum(signal, tables):
    outer_re, outer_im, inner_re, inner_im, twist_re, twist_im = tables
    channels, length = signal.shape
    block_width = inner_re.shape[0]
    half_rows = length // block_width
    blocks = signal.reshape(channels, half_rows, block_width)
    section_re = jnp.einsum("kn,cnm->ckm", outer_re[:, :half_rows], blocks, precision=HIGHEST)
    section_im = jnp.einsum("kn,cnm->ckm", outer_im[:, :half_rows], blocks, precision=HIGHEST)
    turned_re = section_re * twist_re - section_im * twist_im
    turned_im = section_re * twist_im + section_im * twist_re
    frequency_real_component = jnp.matmul(turned_re, inner_re, precision=HIGHEST) - jnp.matmul(
        turned_im, inner_im, precision=HIGHEST
    )
    spec_im = jnp.matmul(turned_re, inner_im, precision=HIGHEST) + jnp.matmul(
        turned_im, inner_re, precision=HIGHEST
    )
    return (frequency_real_component, spec_im)


def inverse(frequency_real_component, spec_im, tables):
    outer_re, outer_im, inner_re, inner_im, twist_re, twist_im = tables
    channels, row_count, block_width = frequency_real_component.shape
    half_rows = row_count // 2
    back_re = jnp.matmul(frequency_real_component, inner_re, precision=HIGHEST) + jnp.matmul(
        spec_im, inner_im, precision=HIGHEST
    )
    back_im = jnp.matmul(spec_im, inner_re, precision=HIGHEST) - jnp.matmul(
        frequency_real_component, inner_im, precision=HIGHEST
    )
    turned_re = back_re * twist_re + back_im * twist_im
    turned_im = back_im * twist_re - back_re * twist_im
    signal = jnp.einsum("nk,ckm->cnm", outer_re[:half_rows], turned_re, precision=HIGHEST)
    signal = signal + jnp.einsum("nk,ckm->cnm", outer_im[:half_rows], turned_im, precision=HIGHEST)
    return (signal / (row_count * block_width)).reshape(channels, half_rows * block_width)


def causal_taps(stacked, earlier, weights):
    tap_count = weights.shape[2]
    length = stacked.shape[2]
    extended = jnp.concatenate([earlier, stacked], axis=2).astype(jnp.float32)
    running_total = jnp.zeros(stacked.shape, jnp.float32)
    for offset in range(tap_count):
        begin = tap_count - 1 - offset
        running_total = (
            running_total
            + weights[:, :, offset : offset + 1] * extended[:, :, begin : begin + length]
        )
    return running_total


def anticausal_taps(stacked, following, weights):
    tap_count = weights.shape[2]
    length = stacked.shape[2]
    extended = jnp.concatenate([stacked, following], axis=2).astype(jnp.float32)
    running_total = jnp.zeros(stacked.shape, jnp.float32)
    for offset in range(tap_count):
        running_total = (
            running_total
            + weights[:, :, offset : offset + 1] * extended[:, :, offset : offset + length]
        )
    return running_total


def to_channels(block):
    return lax.all_to_all(block, CTX, split_axis=0, concat_axis=1, tiled=True)


def to_positions(block):
    return lax.all_to_all(block, CTX, split_axis=1, concat_axis=0, tiled=True)


def swap_layouts(channel_block, position_block):
    count = lax.axis_size(CTX)
    channels, length = channel_block.shape
    local_len = length // count
    outgoing = jnp.stack(
        [
            channel_block.reshape(channels, count, local_len).transpose(1, 0, 2),
            position_block.reshape(count, channels, local_len),
        ],
        axis=1,
    )
    incoming = lax.all_to_all(outgoing, CTX, split_axis=0, concat_axis=0, tiled=True)
    positions = incoming[:, 0].reshape(count * channels, local_len)
    channels_out = incoming[:, 1].transpose(1, 0, 2).reshape(channels, length)
    return positions, channels_out


def weight_gradient(full_cotangent, gated_out):
    hi_count = lax.axis_size(CTX_HI)
    lo_count = lax.axis_size(CTX_LO)
    features, local_len = full_cotangent.shape
    rows = features // (hi_count * lo_count)
    by_target = full_cotangent.reshape(hi_count, lo_count, rows, local_len).transpose(1, 0, 2, 3)
    by_target = by_target.reshape(lo_count, hi_count * rows, local_len)
    outgoing = jnp.concatenate(
        [by_target, jnp.broadcast_to(gated_out, (lo_count,) + gated_out.shape)], axis=1
    )
    incoming = lax.all_to_all(outgoing, CTX_LO, split_axis=0, concat_axis=0, tiled=True)
    group_rows = incoming[:, : hi_count * rows]
    group_gated = incoming[:, hi_count * rows :]
    weight_partial = lax.dot_general(
        group_rows, group_gated, (((0, 2), (0, 2)), ((), ())), preferred_element_type=jnp.float32
    ).astype(jnp.bfloat16)
    weight_partial = weight_partial.reshape(hi_count, rows, gated_out.shape[0])
    received = lax.all_to_all(weight_partial, CTX_HI, split_axis=0, concat_axis=0, tiled=True)
    return received.astype(jnp.float32).sum(0)


def per_device(query_in, key_in, value_in, short_weights, filters, out_weight, cotangent):
    tap_count = short_weights.shape[2]
    local_len = query_in.shape[1]
    stacked = jnp.stack([query_in, key_in, value_in])
    earlier = from_behind(stacked[:, :, local_len - (tap_count - 1) :], CTX, 1)
    shorts = causal_taps(stacked, earlier, short_weights).astype(jnp.bfloat16)
    product = (shorts[1].astype(jnp.float32) * shorts[2].astype(jnp.float32)).astype(jnp.bfloat16)
    product_chan = to_channels(product)
    tables = make_tables(product_chan.shape[1], BLOCK)
    kernel_re, kernel_im = spectrum(filters[0], tables)
    product_re, product_im = spectrum(product_chan.astype(jnp.float32), tables)
    convolved_chan = inverse(
        product_re * kernel_re - product_im * kernel_im,
        product_re * kernel_im + product_im * kernel_re,
        tables,
    ).astype(jnp.bfloat16)
    full_cotangent = lax.all_gather(cotangent, "tp", axis=0, tiled=True)
    grad_gated = lax.dot_general(
        out_weight, full_cotangent, (((0,), (0,)), ((), ())), preferred_element_type=jnp.float32
    )
    grad_conv = (grad_gated * shorts[0].astype(jnp.float32)).astype(jnp.bfloat16)
    convolved, grad_chan = swap_layouts(convolved_chan, grad_conv)
    gated_out = (shorts[0].astype(jnp.float32) * convolved.astype(jnp.float32)).astype(jnp.bfloat16)
    mixed_out = lax.psum_scatter(
        jnp.dot(out_weight, gated_out, preferred_element_type=jnp.float32).astype(jnp.bfloat16),
        "tp",
        scatter_dimension=0,
        tiled=True,
    )
    grad_out_weight = weight_gradient(full_cotangent, gated_out)
    gradient_re, gradient_im = spectrum(grad_chan.astype(jnp.float32), tables)
    grad_product_chan = inverse(
        kernel_re * gradient_re + kernel_im * gradient_im,
        kernel_re * gradient_im - kernel_im * gradient_re,
        tables,
    ).astype(jnp.bfloat16)
    grad_filters = inverse(
        product_re * gradient_re + product_im * gradient_im,
        product_re * gradient_im - product_im * gradient_re,
        tables,
    ).reshape(filters.shape)
    derivative_of_multiple = to_positions(grad_product_chan)
    grad_shorts = jnp.stack(
        [
            grad_gated * convolved.astype(jnp.float32),
            derivative_of_multiple.astype(jnp.float32) * shorts[2].astype(jnp.float32),
            derivative_of_multiple.astype(jnp.float32) * shorts[1].astype(jnp.float32),
        ]
    ).astype(jnp.bfloat16)
    following = from_behind(grad_shorts[:, :, : tap_count - 1], CTX, -1)
    gradients = anticausal_taps(grad_shorts, following, short_weights).astype(jnp.bfloat16)
    return (mixed_out, gradients[0], gradients[1], gradients[2], grad_filters, grad_out_weight)


def solution(mesh):
    ctx_count, tp_count = mesh.devices.shape
    split_mesh = Mesh(
        mesh.devices.reshape(ctx_count // LO_SIZE, LO_SIZE, tp_count), (CTX_HI, CTX_LO, "tp")
    )
    placed = (
        P("tp", CTX),
        P("tp", CTX),
        P("tp", CTX),
        P(None, "tp", None),
        P("tp", CTX, None),
        P(None, "tp"),
        P("tp", CTX),
    )
    return jax.shard_map(
        per_device,
        mesh=split_mesh,
        in_specs=placed,
        out_specs=(
            P("tp", CTX),
            P("tp", CTX),
            P("tp", CTX),
            P("tp", CTX),
            P("tp", CTX, None),
            P(CTX, "tp"),
        ),
        check_vma=False,
    )
```

```python
import math

import jax
import jax.numpy as jnp
from jax import lax
from jax.sharding import Mesh, PartitionSpec as P

BLOCK = 128
CTX_HI = "ctx_hi"
CTX_LO = "ctx_lo"
CTX = (CTX_HI, CTX_LO)
LO_SIZE = 8


TWO_PI = 2.0 * math.pi
HIGHEST = lax.Precision.HIGHEST


def from_behind(value, axis, steps):
    count = lax.axis_size(axis)
    first, last = (max(0, -steps), min(count, count - steps))
    return lax.ppermute(value, axis, [(source, source + steps) for source in range(first, last)])


def fourier_table(count):
    element_indices = jnp.arange(count, dtype=jnp.int32)
    angles = (element_indices[:, None] * element_indices[None, :] % count).astype(jnp.float32) * (
        TWO_PI / count
    )
    return (jnp.cos(angles), -jnp.sin(angles))


def make_tables(length, block_width):
    row_count = 2 * length // block_width
    full_len = row_count * block_width
    outer_re, outer_im = fourier_table(row_count)
    inner_re, inner_im = fourier_table(block_width)
    row_index = jnp.arange(row_count, dtype=jnp.int32)[:, None]
    col_index = jnp.arange(block_width, dtype=jnp.int32)[None, :]
    angles = (row_index * col_index % full_len).astype(jnp.float32) * (TWO_PI / full_len)
    return (outer_re, outer_im, inner_re, inner_im, jnp.cos(angles), -jnp.sin(angles))


def spectrum(signal, tables):
    outer_re, outer_im, inner_re, inner_im, twist_re, twist_im = tables
    channels, length = signal.shape
    block_width = inner_re.shape[0]
    half_rows = length // block_width
    blocks = signal.reshape(channels, half_rows, block_width)
    section_re = jnp.einsum("kn,cnm->ckm", outer_re[:, :half_rows], blocks, precision=HIGHEST)
    section_im = jnp.einsum("kn,cnm->ckm", outer_im[:, :half_rows], blocks, precision=HIGHEST)
    turned_re = section_re * twist_re - section_im * twist_im
    turned_im = section_re * twist_im + section_im * twist_re
    frequency_real_component = jnp.matmul(turned_re, inner_re, precision=HIGHEST) - jnp.matmul(
        turned_im, inner_im, precision=HIGHEST
    )
    spec_im = jnp.matmul(turned_re, inner_im, precision=HIGHEST) + jnp.matmul(
        turned_im, inner_re, precision=HIGHEST
    )
    return (frequency_real_component, spec_im)


def inverse(frequency_real_component, spec_im, tables):
    outer_re, outer_im, inner_re, inner_im, twist_re, twist_im = tables
    channels, row_count, block_width = frequency_real_component.shape
    half_rows = row_count // 2
    back_re = jnp.matmul(frequency_real_component, inner_re, precision=HIGHEST) + jnp.matmul(
        spec_im, inner_im, precision=HIGHEST
    )
    back_im = jnp.matmul(spec_im, inner_re, precision=HIGHEST) - jnp.matmul(
        frequency_real_component, inner_im, precision=HIGHEST
    )
    turned_re = back_re * twist_re + back_im * twist_im
    turned_im = back_im * twist_re - back_re * twist_im
    signal = jnp.einsum("nk,ckm->cnm", outer_re[:half_rows], turned_re, precision=HIGHEST)
    signal = signal + jnp.einsum("nk,ckm->cnm", outer_im[:half_rows], turned_im, precision=HIGHEST)
    return (signal / (row_count * block_width)).reshape(channels, half_rows * block_width)


def causal_taps(stacked, earlier, weights):
    tap_count = weights.shape[2]
    length = stacked.shape[2]
    extended = jnp.concatenate([earlier, stacked], axis=2).astype(jnp.float32)
    running_total = jnp.zeros(stacked.shape, jnp.float32)
    for offset in range(tap_count):
        begin = tap_count - 1 - offset
        running_total = (
            running_total
            + weights[:, :, offset : offset + 1] * extended[:, :, begin : begin + length]
        )
    return running_total


def anticausal_taps(stacked, following, weights):
    tap_count = weights.shape[2]
    length = stacked.shape[2]
    extended = jnp.concatenate([stacked, following], axis=2).astype(jnp.float32)
    running_total = jnp.zeros(stacked.shape, jnp.float32)
    for offset in range(tap_count):
        running_total = (
            running_total
            + weights[:, :, offset : offset + 1] * extended[:, :, offset : offset + length]
        )
    return running_total


def to_channels(block):
    return lax.all_to_all(block, CTX, split_axis=0, concat_axis=1, tiled=True)


def to_positions(block):
    return lax.all_to_all(block, CTX, split_axis=1, concat_axis=0, tiled=True)


def swap_layouts(channel_block, position_block):
    count = lax.axis_size(CTX)
    channels, length = channel_block.shape
    local_len = length // count
    outgoing = jnp.stack(
        [
            channel_block.reshape(channels, count, local_len).transpose(1, 0, 2),
            position_block.reshape(count, channels, local_len),
        ],
        axis=1,
    )
    incoming = lax.all_to_all(outgoing, CTX, split_axis=0, concat_axis=0, tiled=True)
    positions = incoming[:, 0].reshape(count * channels, local_len)
    channels_out = incoming[:, 1].transpose(1, 0, 2).reshape(channels, length)
    return positions, channels_out


def weight_gradient(full_cotangent, gated_out):
    hi_count = lax.axis_size(CTX_HI)
    lo_count = lax.axis_size(CTX_LO)
    features, local_len = full_cotangent.shape
    rows = features // (hi_count * lo_count)
    by_target = full_cotangent.reshape(hi_count, lo_count, rows, local_len).transpose(1, 0, 2, 3)
    by_target = by_target.reshape(lo_count, hi_count * rows, local_len)
    outgoing = jnp.concatenate(
        [by_target, jnp.broadcast_to(gated_out, (lo_count,) + gated_out.shape)], axis=1
    )
    incoming = lax.all_to_all(outgoing, CTX_LO, split_axis=0, concat_axis=0, tiled=True)
    group_rows = incoming[:, : hi_count * rows]
    group_gated = incoming[:, hi_count * rows :]
    weight_partial = lax.dot_general(
        group_rows, group_gated, (((0, 2), (0, 2)), ((), ())), preferred_element_type=jnp.float32
    ).astype(jnp.bfloat16)
    weight_partial = weight_partial.reshape(hi_count, rows, gated_out.shape[0])
    received = lax.all_to_all(weight_partial, CTX_HI, split_axis=0, concat_axis=0, tiled=True)
    return received.astype(jnp.float32).sum(0)


def per_device(query_in, key_in, value_in, short_weights, filters, out_weight, cotangent):
    tap_count = short_weights.shape[2]
    local_len = query_in.shape[1]
    stacked = jnp.stack([query_in, key_in, value_in])
    earlier = from_behind(stacked[:, :, local_len - (tap_count - 1) :], CTX, 1)
    shorts = causal_taps(stacked, earlier, short_weights).astype(jnp.bfloat16)
    product = (shorts[1].astype(jnp.float32) * shorts[2].astype(jnp.float32)).astype(jnp.bfloat16)
    product_chan = to_channels(product)
    tables = make_tables(product_chan.shape[1], BLOCK)
    kernel_re, kernel_im = spectrum(filters[0], tables)
    product_re, product_im = spectrum(product_chan.astype(jnp.float32), tables)
    convolved_chan = inverse(
        product_re * kernel_re - product_im * kernel_im,
        product_re * kernel_im + product_im * kernel_re,
        tables,
    ).astype(jnp.bfloat16)
    full_cotangent = lax.all_gather(cotangent, "tp", axis=0, tiled=True)
    grad_gated = lax.dot_general(
        out_weight, full_cotangent, (((0,), (0,)), ((), ())), preferred_element_type=jnp.float32
    )
    grad_conv = (grad_gated * shorts[0].astype(jnp.float32)).astype(jnp.bfloat16)
    convolved, grad_chan = swap_layouts(convolved_chan, grad_conv)
    gated_out = (shorts[0].astype(jnp.float32) * convolved.astype(jnp.float32)).astype(jnp.bfloat16)
    tp_count = lax.axis_size("tp")
    mixed_partial = jnp.dot(out_weight, gated_out, preferred_element_type=jnp.float32)
    mixed_partial = mixed_partial.astype(jnp.bfloat16).reshape(tp_count, -1, gated_out.shape[1])
    mixed_out = lax.all_to_all(mixed_partial, "tp", split_axis=0, concat_axis=0, tiled=True)
    mixed_out = mixed_out.astype(jnp.float32).sum(0).astype(jnp.bfloat16)
    grad_out_weight = weight_gradient(full_cotangent, gated_out)
    gradient_re, gradient_im = spectrum(grad_chan.astype(jnp.float32), tables)
    grad_product_chan = inverse(
        kernel_re * gradient_re + kernel_im * gradient_im,
        kernel_re * gradient_im - kernel_im * gradient_re,
        tables,
    ).astype(jnp.bfloat16)
    grad_filters = inverse(
        product_re * gradient_re + product_im * gradient_im,
        product_re * gradient_im - product_im * gradient_re,
        tables,
    ).reshape(filters.shape)
    derivative_of_multiple = to_positions(grad_product_chan)
    grad_shorts = jnp.stack(
        [
            grad_gated * convolved.astype(jnp.float32),
            derivative_of_multiple.astype(jnp.float32) * shorts[2].astype(jnp.float32),
            derivative_of_multiple.astype(jnp.float32) * shorts[1].astype(jnp.float32),
        ]
    ).astype(jnp.bfloat16)
    following = from_behind(grad_shorts[:, :, : tap_count - 1], CTX, -1)
    gradients = anticausal_taps(grad_shorts, following, short_weights).astype(jnp.bfloat16)
    return (mixed_out, gradients[0], gradients[1], gradients[2], grad_filters, grad_out_weight)


def solution(mesh):
    ctx_count, tp_count = mesh.devices.shape
    split_mesh = Mesh(
        mesh.devices.reshape(ctx_count // LO_SIZE, LO_SIZE, tp_count), (CTX_HI, CTX_LO, "tp")
    )
    placed = (
        P("tp", CTX),
        P("tp", CTX),
        P("tp", CTX),
        P(None, "tp", None),
        P("tp", CTX, None),
        P(None, "tp"),
        P("tp", CTX),
    )
    return jax.shard_map(
        per_device,
        mesh=split_mesh,
        in_specs=placed,
        out_specs=(
            P("tp", CTX),
            P("tp", CTX),
            P("tp", CTX),
            P("tp", CTX),
            P("tp", CTX, None),
            P(CTX, "tp"),
        ),
        check_vma=False,
    )
```

```python
import math

import jax
import jax.numpy as jnp
from jax import lax
from jax.sharding import Mesh, PartitionSpec as P

BLOCK = 128
CTX_HI = "ctx_hi"
CTX_LO = "ctx_lo"
CTX = (CTX_HI, CTX_LO)
LO_SIZE = 8


TWO_PI = 2.0 * math.pi
HIGHEST = lax.Precision.HIGHEST


def from_behind(value, axis, steps):
    count = lax.axis_size(axis)
    first, last = (max(0, -steps), min(count, count - steps))
    return lax.ppermute(value, axis, [(source, source + steps) for source in range(first, last)])


def fourier_table(count):
    element_indices = jnp.arange(count, dtype=jnp.int32)
    angles = (element_indices[:, None] * element_indices[None, :] % count).astype(jnp.float32) * (
        TWO_PI / count
    )
    return (jnp.cos(angles), -jnp.sin(angles))


def make_tables(length, block_width):
    row_count = 2 * length // block_width
    full_len = row_count * block_width
    outer_re, outer_im = fourier_table(row_count)
    inner_re, inner_im = fourier_table(block_width)
    row_index = jnp.arange(row_count, dtype=jnp.int32)[:, None]
    col_index = jnp.arange(block_width, dtype=jnp.int32)[None, :]
    angles = (row_index * col_index % full_len).astype(jnp.float32) * (TWO_PI / full_len)
    return (outer_re, outer_im, inner_re, inner_im, jnp.cos(angles), -jnp.sin(angles))


def spectrum(signal, tables):
    outer_re, outer_im, inner_re, inner_im, twist_re, twist_im = tables
    channels, length = signal.shape
    block_width = inner_re.shape[0]
    half_rows = length // block_width
    blocks = signal.reshape(channels, half_rows, block_width)
    section_re = jnp.einsum("kn,cnm->ckm", outer_re[:, :half_rows], blocks, precision=HIGHEST)
    section_im = jnp.einsum("kn,cnm->ckm", outer_im[:, :half_rows], blocks, precision=HIGHEST)
    turned_re = section_re * twist_re - section_im * twist_im
    turned_im = section_re * twist_im + section_im * twist_re
    frequency_real_component = jnp.matmul(turned_re, inner_re, precision=HIGHEST) - jnp.matmul(
        turned_im, inner_im, precision=HIGHEST
    )
    spec_im = jnp.matmul(turned_re, inner_im, precision=HIGHEST) + jnp.matmul(
        turned_im, inner_re, precision=HIGHEST
    )
    return (frequency_real_component, spec_im)


def inverse(frequency_real_component, spec_im, tables):
    outer_re, outer_im, inner_re, inner_im, twist_re, twist_im = tables
    channels, row_count, block_width = frequency_real_component.shape
    half_rows = row_count // 2
    back_re = jnp.matmul(frequency_real_component, inner_re, precision=HIGHEST) + jnp.matmul(
        spec_im, inner_im, precision=HIGHEST
    )
    back_im = jnp.matmul(spec_im, inner_re, precision=HIGHEST) - jnp.matmul(
        frequency_real_component, inner_im, precision=HIGHEST
    )
    turned_re = back_re * twist_re + back_im * twist_im
    turned_im = back_im * twist_re - back_re * twist_im
    signal = jnp.einsum("nk,ckm->cnm", outer_re[:half_rows], turned_re, precision=HIGHEST)
    signal = signal + jnp.einsum("nk,ckm->cnm", outer_im[:half_rows], turned_im, precision=HIGHEST)
    return (signal / (row_count * block_width)).reshape(channels, half_rows * block_width)


def causal_taps(stacked, earlier, weights):
    tap_count = weights.shape[2]
    length = stacked.shape[2]
    extended = jnp.concatenate([earlier, stacked], axis=2).astype(jnp.float32)
    running_total = jnp.zeros(stacked.shape, jnp.float32)
    for offset in range(tap_count):
        begin = tap_count - 1 - offset
        running_total = (
            running_total
            + weights[:, :, offset : offset + 1] * extended[:, :, begin : begin + length]
        )
    return running_total


def anticausal_taps(stacked, following, weights):
    tap_count = weights.shape[2]
    length = stacked.shape[2]
    extended = jnp.concatenate([stacked, following], axis=2).astype(jnp.float32)
    running_total = jnp.zeros(stacked.shape, jnp.float32)
    for offset in range(tap_count):
        running_total = (
            running_total
            + weights[:, :, offset : offset + 1] * extended[:, :, offset : offset + length]
        )
    return running_total


def to_channels(block):
    return lax.all_to_all(block, CTX, split_axis=0, concat_axis=1, tiled=True)


def to_positions(block):
    return lax.all_to_all(block, CTX, split_axis=1, concat_axis=0, tiled=True)


def swap_layouts(channel_block, position_block):
    count = lax.axis_size(CTX)
    channels, length = channel_block.shape
    local_len = length // count
    outgoing = jnp.stack(
        [
            channel_block.reshape(channels, count, local_len).transpose(1, 0, 2),
            position_block.reshape(count, channels, local_len),
        ],
        axis=1,
    )
    incoming = lax.all_to_all(outgoing, CTX, split_axis=0, concat_axis=0, tiled=True)
    positions = incoming[:, 0].reshape(count * channels, local_len)
    channels_out = incoming[:, 1].transpose(1, 0, 2).reshape(channels, length)
    return positions, channels_out


def weight_gradient(full_cotangent, gated_out, finished_first):
    hi_count = lax.axis_size(CTX_HI)
    lo_count = lax.axis_size(CTX_LO)
    features, local_len = full_cotangent.shape
    rows = features // (hi_count * lo_count)
    by_target = full_cotangent.reshape(hi_count, lo_count, rows, local_len).transpose(1, 0, 2, 3)
    by_target = by_target.reshape(lo_count, hi_count * rows, local_len)
    outgoing = jnp.concatenate(
        [by_target, jnp.broadcast_to(gated_out, (lo_count,) + gated_out.shape)], axis=1
    )
    outgoing, finished_first = lax.optimization_barrier((outgoing, finished_first))
    incoming = lax.all_to_all(outgoing, CTX_LO, split_axis=0, concat_axis=0, tiled=True)
    group_rows = incoming[:, : hi_count * rows]
    group_gated = incoming[:, hi_count * rows :]
    weight_partial = lax.dot_general(
        group_rows, group_gated, (((0, 2), (0, 2)), ((), ())), preferred_element_type=jnp.float32
    ).astype(jnp.bfloat16)
    weight_partial = weight_partial.reshape(hi_count, rows, gated_out.shape[0])
    received = lax.all_to_all(weight_partial, CTX_HI, split_axis=0, concat_axis=0, tiled=True)
    return received.astype(jnp.float32).sum(0), finished_first


def per_device(query_in, key_in, value_in, short_weights, filters, out_weight, cotangent):
    tap_count = short_weights.shape[2]
    local_len = query_in.shape[1]
    stacked = jnp.stack([query_in, key_in, value_in])
    earlier = from_behind(stacked[:, :, local_len - (tap_count - 1) :], CTX, 1)
    shorts = causal_taps(stacked, earlier, short_weights).astype(jnp.bfloat16)
    product = (shorts[1].astype(jnp.float32) * shorts[2].astype(jnp.float32)).astype(jnp.bfloat16)
    product_chan = to_channels(product)
    tables = make_tables(product_chan.shape[1], BLOCK)
    kernel_re, kernel_im = spectrum(filters[0], tables)
    product_re, product_im = spectrum(product_chan.astype(jnp.float32), tables)
    convolved_chan = inverse(
        product_re * kernel_re - product_im * kernel_im,
        product_re * kernel_im + product_im * kernel_re,
        tables,
    ).astype(jnp.bfloat16)
    full_cotangent = lax.all_gather(cotangent, "tp", axis=0, tiled=True)
    grad_gated = lax.dot_general(
        out_weight, full_cotangent, (((0,), (0,)), ((), ())), preferred_element_type=jnp.float32
    )
    grad_conv = (grad_gated * shorts[0].astype(jnp.float32)).astype(jnp.bfloat16)
    convolved, grad_chan = swap_layouts(convolved_chan, grad_conv)
    gated_out = (shorts[0].astype(jnp.float32) * convolved.astype(jnp.float32)).astype(jnp.bfloat16)
    mixed_out = lax.psum_scatter(
        jnp.dot(out_weight, gated_out, preferred_element_type=jnp.float32).astype(jnp.bfloat16),
        "tp",
        scatter_dimension=0,
        tiled=True,
    )
    grad_out_weight, mixed_out = weight_gradient(full_cotangent, gated_out, mixed_out)
    gradient_re, gradient_im = spectrum(grad_chan.astype(jnp.float32), tables)
    grad_product_chan = inverse(
        kernel_re * gradient_re + kernel_im * gradient_im,
        kernel_re * gradient_im - kernel_im * gradient_re,
        tables,
    ).astype(jnp.bfloat16)
    grad_filters = inverse(
        product_re * gradient_re + product_im * gradient_im,
        product_re * gradient_im - product_im * gradient_re,
        tables,
    ).reshape(filters.shape)
    derivative_of_multiple = to_positions(grad_product_chan)
    grad_shorts = jnp.stack(
        [
            grad_gated * convolved.astype(jnp.float32),
            derivative_of_multiple.astype(jnp.float32) * shorts[2].astype(jnp.float32),
            derivative_of_multiple.astype(jnp.float32) * shorts[1].astype(jnp.float32),
        ]
    ).astype(jnp.bfloat16)
    following = from_behind(grad_shorts[:, :, : tap_count - 1], CTX, -1)
    gradients = anticausal_taps(grad_shorts, following, short_weights).astype(jnp.bfloat16)
    return (mixed_out, gradients[0], gradients[1], gradients[2], grad_filters, grad_out_weight)


def solution(mesh):
    ctx_count, tp_count = mesh.devices.shape
    split_mesh = Mesh(
        mesh.devices.reshape(ctx_count // LO_SIZE, LO_SIZE, tp_count), (CTX_HI, CTX_LO, "tp")
    )
    placed = (
        P("tp", CTX),
        P("tp", CTX),
        P("tp", CTX),
        P(None, "tp", None),
        P("tp", CTX, None),
        P(None, "tp"),
        P("tp", CTX),
    )
    return jax.shard_map(
        per_device,
        mesh=split_mesh,
        in_specs=placed,
        out_specs=(
            P("tp", CTX),
            P("tp", CTX),
            P("tp", CTX),
            P("tp", CTX),
            P("tp", CTX, None),
            P(CTX, "tp"),
        ),
        check_vma=False,
    )
```

```python
import math

import jax
import jax.numpy as jnp
from jax import lax
from jax.sharding import Mesh, PartitionSpec as P

BLOCK = 128
CTX_HI = "ctx_hi"
CTX_LO = "ctx_lo"
CTX = (CTX_HI, CTX_LO)
LO_SIZE = 8


TWO_PI = 2.0 * math.pi
DFT_PRECISION = lax.Precision.HIGH


def from_behind(value, axis, steps):
    count = lax.axis_size(axis)
    first, last = (max(0, -steps), min(count, count - steps))
    return lax.ppermute(value, axis, [(source, source + steps) for source in range(first, last)])


def fourier_table(count):
    element_indices = jnp.arange(count, dtype=jnp.int32)
    angles = (element_indices[:, None] * element_indices[None, :] % count).astype(jnp.float32) * (
        TWO_PI / count
    )
    return (jnp.cos(angles), -jnp.sin(angles))


def make_tables(length, block_width):
    row_count = 2 * length // block_width
    full_len = row_count * block_width
    outer_re, outer_im = fourier_table(row_count)
    inner_re, inner_im = fourier_table(block_width)
    row_index = jnp.arange(row_count, dtype=jnp.int32)[:, None]
    col_index = jnp.arange(block_width, dtype=jnp.int32)[None, :]
    angles = (row_index * col_index % full_len).astype(jnp.float32) * (TWO_PI / full_len)
    return (outer_re, outer_im, inner_re, inner_im, jnp.cos(angles), -jnp.sin(angles))


def spectrum(signal, tables):
    outer_re, outer_im, inner_re, inner_im, twist_re, twist_im = tables
    channels, length = signal.shape
    block_width = inner_re.shape[0]
    half_rows = length // block_width
    blocks = signal.reshape(channels, half_rows, block_width)
    section_re = jnp.einsum("kn,cnm->ckm", outer_re[:, :half_rows], blocks, precision=DFT_PRECISION)
    section_im = jnp.einsum("kn,cnm->ckm", outer_im[:, :half_rows], blocks, precision=DFT_PRECISION)
    turned_re = section_re * twist_re - section_im * twist_im
    turned_im = section_re * twist_im + section_im * twist_re
    frequency_real_component = jnp.matmul(turned_re, inner_re, precision=DFT_PRECISION) - jnp.matmul(
        turned_im, inner_im, precision=DFT_PRECISION
    )
    spec_im = jnp.matmul(turned_re, inner_im, precision=DFT_PRECISION) + jnp.matmul(
        turned_im, inner_re, precision=DFT_PRECISION
    )
    return (frequency_real_component, spec_im)


def inverse(frequency_real_component, spec_im, tables):
    outer_re, outer_im, inner_re, inner_im, twist_re, twist_im = tables
    channels, row_count, block_width = frequency_real_component.shape
    half_rows = row_count // 2
    back_re = jnp.matmul(frequency_real_component, inner_re, precision=DFT_PRECISION) + jnp.matmul(
        spec_im, inner_im, precision=DFT_PRECISION
    )
    back_im = jnp.matmul(spec_im, inner_re, precision=DFT_PRECISION) - jnp.matmul(
        frequency_real_component, inner_im, precision=DFT_PRECISION
    )
    turned_re = back_re * twist_re + back_im * twist_im
    turned_im = back_im * twist_re - back_re * twist_im
    signal = jnp.einsum("nk,ckm->cnm", outer_re[:half_rows], turned_re, precision=DFT_PRECISION)
    signal = signal + jnp.einsum("nk,ckm->cnm", outer_im[:half_rows], turned_im, precision=DFT_PRECISION)
    return (signal / (row_count * block_width)).reshape(channels, half_rows * block_width)


def causal_taps(stacked, earlier, weights):
    tap_count = weights.shape[2]
    length = stacked.shape[2]
    extended = jnp.concatenate([earlier, stacked], axis=2).astype(jnp.float32)
    running_total = jnp.zeros(stacked.shape, jnp.float32)
    for offset in range(tap_count):
        begin = tap_count - 1 - offset
        running_total = (
            running_total
            + weights[:, :, offset : offset + 1] * extended[:, :, begin : begin + length]
        )
    return running_total


def anticausal_taps(stacked, following, weights):
    tap_count = weights.shape[2]
    length = stacked.shape[2]
    extended = jnp.concatenate([stacked, following], axis=2).astype(jnp.float32)
    running_total = jnp.zeros(stacked.shape, jnp.float32)
    for offset in range(tap_count):
        running_total = (
            running_total
            + weights[:, :, offset : offset + 1] * extended[:, :, offset : offset + length]
        )
    return running_total


def to_channels(block):
    return lax.all_to_all(block, CTX, split_axis=0, concat_axis=1, tiled=True)


def to_positions(block):
    return lax.all_to_all(block, CTX, split_axis=1, concat_axis=0, tiled=True)


def swap_layouts(channel_block, position_block):
    count = lax.axis_size(CTX)
    channels, length = channel_block.shape
    local_len = length // count
    outgoing = jnp.stack(
        [
            channel_block.reshape(channels, count, local_len).transpose(1, 0, 2),
            position_block.reshape(count, channels, local_len),
        ],
        axis=1,
    )
    incoming = lax.all_to_all(outgoing, CTX, split_axis=0, concat_axis=0, tiled=True)
    positions = incoming[:, 0].reshape(count * channels, local_len)
    channels_out = incoming[:, 1].transpose(1, 0, 2).reshape(channels, length)
    return positions, channels_out


def weight_gradient(full_cotangent, gated_out):
    hi_count = lax.axis_size(CTX_HI)
    lo_count = lax.axis_size(CTX_LO)
    features, local_len = full_cotangent.shape
    rows = features // (hi_count * lo_count)
    group_gated = lax.all_gather(gated_out, CTX_LO, axis=1, tiled=True)
    group_gated = group_gated.reshape(gated_out.shape[0], lo_count, local_len)
    by_target = full_cotangent.reshape(hi_count, lo_count, rows, local_len).transpose(1, 0, 2, 3)
    group_rows = lax.all_to_all(by_target, CTX_LO, split_axis=0, concat_axis=0, tiled=True)
    weight_partial = lax.dot_general(
        group_rows, group_gated, (((0, 3), (1, 2)), ((), ())), preferred_element_type=jnp.float32
    ).astype(jnp.bfloat16)
    received = lax.all_to_all(weight_partial, CTX_HI, split_axis=0, concat_axis=0, tiled=True)
    return received.astype(jnp.float32).sum(0)


def per_device(query_in, key_in, value_in, short_weights, filters, out_weight, cotangent):
    tap_count = short_weights.shape[2]
    local_len = query_in.shape[1]
    stacked = jnp.stack([query_in, key_in, value_in])
    earlier = from_behind(stacked[:, :, local_len - (tap_count - 1) :], CTX, 1)
    shorts = causal_taps(stacked, earlier, short_weights).astype(jnp.bfloat16)
    product = (shorts[1].astype(jnp.float32) * shorts[2].astype(jnp.float32)).astype(jnp.bfloat16)
    product_chan = to_channels(product)
    tables = make_tables(product_chan.shape[1], BLOCK)
    kernel_re, kernel_im = spectrum(filters[0], tables)
    product_re, product_im = spectrum(product_chan.astype(jnp.float32), tables)
    convolved_chan = inverse(
        product_re * kernel_re - product_im * kernel_im,
        product_re * kernel_im + product_im * kernel_re,
        tables,
    ).astype(jnp.bfloat16)
    full_cotangent = lax.all_gather(cotangent, "tp", axis=0, tiled=True)
    grad_gated = lax.dot_general(
        out_weight, full_cotangent, (((0,), (0,)), ((), ())), preferred_element_type=jnp.float32
    )
    grad_conv = (grad_gated * shorts[0].astype(jnp.float32)).astype(jnp.bfloat16)
    convolved, grad_chan = swap_layouts(convolved_chan, grad_conv)
    gated_out = (shorts[0].astype(jnp.float32) * convolved.astype(jnp.float32)).astype(jnp.bfloat16)
    mixed_out = lax.psum_scatter(
        jnp.dot(out_weight, gated_out, preferred_element_type=jnp.float32).astype(jnp.bfloat16),
        "tp",
        scatter_dimension=0,
        tiled=True,
    )
    grad_out_weight = weight_gradient(full_cotangent, gated_out)
    gradient_re, gradient_im = spectrum(grad_chan.astype(jnp.float32), tables)
    grad_product_chan = inverse(
        kernel_re * gradient_re + kernel_im * gradient_im,
        kernel_re * gradient_im - kernel_im * gradient_re,
        tables,
    ).astype(jnp.bfloat16)
    grad_filters = inverse(
        product_re * gradient_re + product_im * gradient_im,
        product_re * gradient_im - product_im * gradient_re,
        tables,
    ).reshape(filters.shape)
    derivative_of_multiple = to_positions(grad_product_chan)
    grad_shorts = jnp.stack(
        [
            grad_gated * convolved.astype(jnp.float32),
            derivative_of_multiple.astype(jnp.float32) * shorts[2].astype(jnp.float32),
            derivative_of_multiple.astype(jnp.float32) * shorts[1].astype(jnp.float32),
        ]
    ).astype(jnp.bfloat16)
    following = from_behind(grad_shorts[:, :, : tap_count - 1], CTX, -1)
    gradients = anticausal_taps(grad_shorts, following, short_weights).astype(jnp.bfloat16)
    return (mixed_out, gradients[0], gradients[1], gradients[2], grad_filters, grad_out_weight)


def solution(mesh):
    ctx_count, tp_count = mesh.devices.shape
    split_mesh = Mesh(
        mesh.devices.reshape(ctx_count // LO_SIZE, LO_SIZE, tp_count), (CTX_HI, CTX_LO, "tp")
    )
    placed = (
        P("tp", CTX),
        P("tp", CTX),
        P("tp", CTX),
        P(None, "tp", None),
        P("tp", CTX, None),
        P(None, "tp"),
        P("tp", CTX),
    )
    return jax.shard_map(
        per_device,
        mesh=split_mesh,
        in_specs=placed,
        out_specs=(
            P("tp", CTX),
            P("tp", CTX),
            P("tp", CTX),
            P("tp", CTX),
            P("tp", CTX, None),
            P(CTX, "tp"),
        ),
        check_vma=False,
    )
```

```python
import math

import jax
import jax.numpy as jnp
from jax import lax
from jax.sharding import Mesh, PartitionSpec as P

BLOCK = 128
CTX_HI = "ctx_hi"
CTX_LO = "ctx_lo"
CTX = (CTX_HI, CTX_LO)
LO_SIZE = 8


TWO_PI = 2.0 * math.pi
DFT_PRECISION = lax.Precision.HIGH


def from_behind(value, axis, steps):
    count = lax.axis_size(axis)
    first, last = (max(0, -steps), min(count, count - steps))
    return lax.ppermute(value, axis, [(source, source + steps) for source in range(first, last)])


def fourier_table(count):
    element_indices = jnp.arange(count, dtype=jnp.int32)
    angles = (element_indices[:, None] * element_indices[None, :] % count).astype(jnp.float32) * (
        TWO_PI / count
    )
    return (jnp.cos(angles), -jnp.sin(angles))


def make_tables(length, block_width):
    row_count = 2 * length // block_width
    full_len = row_count * block_width
    outer_re, outer_im = fourier_table(row_count)
    inner_re, inner_im = fourier_table(block_width)
    row_index = jnp.arange(row_count, dtype=jnp.int32)[:, None]
    col_index = jnp.arange(block_width, dtype=jnp.int32)[None, :]
    angles = (row_index * col_index % full_len).astype(jnp.float32) * (TWO_PI / full_len)
    return (outer_re, outer_im, inner_re, inner_im, jnp.cos(angles), -jnp.sin(angles))


def spectrum(signal, tables):
    outer_re, outer_im, inner_re, inner_im, twist_re, twist_im = tables
    channels, length = signal.shape
    block_width = inner_re.shape[0]
    half_rows = length // block_width
    blocks = signal.reshape(channels, half_rows, block_width)
    section_re = jnp.einsum("kn,cnm->ckm", outer_re[:, :half_rows], blocks, precision=DFT_PRECISION)
    section_im = jnp.einsum("kn,cnm->ckm", outer_im[:, :half_rows], blocks, precision=DFT_PRECISION)
    turned_re = section_re * twist_re - section_im * twist_im
    turned_im = section_re * twist_im + section_im * twist_re
    frequency_real_component = jnp.matmul(turned_re, inner_re, precision=DFT_PRECISION) - jnp.matmul(
        turned_im, inner_im, precision=DFT_PRECISION
    )
    spec_im = jnp.matmul(turned_re, inner_im, precision=DFT_PRECISION) + jnp.matmul(
        turned_im, inner_re, precision=DFT_PRECISION
    )
    return (frequency_real_component, spec_im)


def inverse(frequency_real_component, spec_im, tables):
    outer_re, outer_im, inner_re, inner_im, twist_re, twist_im = tables
    channels, row_count, block_width = frequency_real_component.shape
    half_rows = row_count // 2
    back_re = jnp.matmul(frequency_real_component, inner_re, precision=DFT_PRECISION) + jnp.matmul(
        spec_im, inner_im, precision=DFT_PRECISION
    )
    back_im = jnp.matmul(spec_im, inner_re, precision=DFT_PRECISION) - jnp.matmul(
        frequency_real_component, inner_im, precision=DFT_PRECISION
    )
    turned_re = back_re * twist_re + back_im * twist_im
    turned_im = back_im * twist_re - back_re * twist_im
    signal = jnp.einsum("nk,ckm->cnm", outer_re[:half_rows], turned_re, precision=DFT_PRECISION)
    signal = signal + jnp.einsum("nk,ckm->cnm", outer_im[:half_rows], turned_im, precision=DFT_PRECISION)
    return (signal / (row_count * block_width)).reshape(channels, half_rows * block_width)


def causal_taps(stacked, earlier, weights):
    tap_count = weights.shape[2]
    length = stacked.shape[2]
    extended = jnp.concatenate([earlier, stacked], axis=2).astype(jnp.float32)
    running_total = jnp.zeros(stacked.shape, jnp.float32)
    for offset in range(tap_count):
        begin = tap_count - 1 - offset
        running_total = (
            running_total
            + weights[:, :, offset : offset + 1] * extended[:, :, begin : begin + length]
        )
    return running_total


def anticausal_taps(stacked, following, weights):
    tap_count = weights.shape[2]
    length = stacked.shape[2]
    extended = jnp.concatenate([stacked, following], axis=2).astype(jnp.float32)
    running_total = jnp.zeros(stacked.shape, jnp.float32)
    for offset in range(tap_count):
        running_total = (
            running_total
            + weights[:, :, offset : offset + 1] * extended[:, :, offset : offset + length]
        )
    return running_total


def to_channels(block):
    return lax.all_to_all(block, CTX, split_axis=0, concat_axis=1, tiled=True)


def to_positions(block):
    return lax.all_to_all(block, CTX, split_axis=1, concat_axis=0, tiled=True)


def swap_layouts(channel_block, position_block):
    count = lax.axis_size(CTX)
    channels, length = channel_block.shape
    local_len = length // count
    outgoing = jnp.stack(
        [
            channel_block.reshape(channels, count, local_len).transpose(1, 0, 2),
            position_block.reshape(count, channels, local_len),
        ],
        axis=1,
    )
    incoming = lax.all_to_all(outgoing, CTX, split_axis=0, concat_axis=0, tiled=True)
    positions = incoming[:, 0].reshape(count * channels, local_len)
    channels_out = incoming[:, 1].transpose(1, 0, 2).reshape(channels, length)
    return positions, channels_out


def weight_gradient(full_cotangent, gated_out):
    hi_count = lax.axis_size(CTX_HI)
    lo_count = lax.axis_size(CTX_LO)
    features, local_len = full_cotangent.shape
    rows = features // (hi_count * lo_count)
    group_gated = lax.all_gather(gated_out, CTX_LO, axis=1, tiled=True)
    group_gated = group_gated.reshape(gated_out.shape[0], lo_count, local_len)
    by_target = full_cotangent.reshape(hi_count, lo_count, rows, local_len).transpose(1, 0, 2, 3)
    group_rows = lax.all_to_all(by_target, CTX_LO, split_axis=0, concat_axis=0, tiled=True)
    weight_partial = lax.dot_general(
        group_rows, group_gated, (((0, 3), (1, 2)), ((), ())), preferred_element_type=jnp.float32
    ).astype(jnp.bfloat16)
    received = lax.all_to_all(weight_partial, CTX_HI, split_axis=0, concat_axis=0, tiled=True)
    return received.astype(jnp.float32).sum(0)


def per_device(query_in, key_in, value_in, short_weights, filters, out_weight, cotangent):
    tap_count = short_weights.shape[2]
    local_len = query_in.shape[1]
    stacked = jnp.stack([query_in, key_in, value_in])
    earlier = from_behind(stacked[:, :, local_len - (tap_count - 1) :], CTX, 1)
    shorts = causal_taps(stacked, earlier, short_weights).astype(jnp.bfloat16)
    product = (shorts[1].astype(jnp.float32) * shorts[2].astype(jnp.float32)).astype(jnp.bfloat16)
    product_chan = to_channels(product)
    tables = make_tables(product_chan.shape[1], BLOCK)
    channels = product_chan.shape[0]
    joint_re, joint_im = spectrum(
        jnp.concatenate([filters[0], product_chan.astype(jnp.float32)]), tables
    )
    kernel_re, product_re = joint_re[:channels], joint_re[channels:]
    kernel_im, product_im = joint_im[:channels], joint_im[channels:]
    convolved_chan = inverse(
        product_re * kernel_re - product_im * kernel_im,
        product_re * kernel_im + product_im * kernel_re,
        tables,
    ).astype(jnp.bfloat16)
    full_cotangent = lax.all_gather(cotangent, "tp", axis=0, tiled=True)
    grad_gated = lax.dot_general(
        out_weight, full_cotangent, (((0,), (0,)), ((), ())), preferred_element_type=jnp.float32
    )
    grad_conv = (grad_gated * shorts[0].astype(jnp.float32)).astype(jnp.bfloat16)
    convolved, grad_chan = swap_layouts(convolved_chan, grad_conv)
    gated_out = (shorts[0].astype(jnp.float32) * convolved.astype(jnp.float32)).astype(jnp.bfloat16)
    mixed_out = lax.psum_scatter(
        jnp.dot(out_weight, gated_out, preferred_element_type=jnp.float32).astype(jnp.bfloat16),
        "tp",
        scatter_dimension=0,
        tiled=True,
    )
    grad_out_weight = weight_gradient(full_cotangent, gated_out)
    gradient_re, gradient_im = spectrum(grad_chan.astype(jnp.float32), tables)
    pair = inverse(
        jnp.concatenate(
            [
                kernel_re * gradient_re + kernel_im * gradient_im,
                product_re * gradient_re + product_im * gradient_im,
            ]
        ),
        jnp.concatenate(
            [
                kernel_re * gradient_im - kernel_im * gradient_re,
                product_re * gradient_im - product_im * gradient_re,
            ]
        ),
        tables,
    )
    grad_product_chan = pair[:channels].astype(jnp.bfloat16)
    grad_filters = pair[channels:].reshape(filters.shape)
    derivative_of_multiple = to_positions(grad_product_chan)
    grad_shorts = jnp.stack(
        [
            grad_gated * convolved.astype(jnp.float32),
            derivative_of_multiple.astype(jnp.float32) * shorts[2].astype(jnp.float32),
            derivative_of_multiple.astype(jnp.float32) * shorts[1].astype(jnp.float32),
        ]
    ).astype(jnp.bfloat16)
    following = from_behind(grad_shorts[:, :, : tap_count - 1], CTX, -1)
    gradients = anticausal_taps(grad_shorts, following, short_weights).astype(jnp.bfloat16)
    return (mixed_out, gradients[0], gradients[1], gradients[2], grad_filters, grad_out_weight)


def solution(mesh):
    ctx_count, tp_count = mesh.devices.shape
    split_mesh = Mesh(
        mesh.devices.reshape(ctx_count // LO_SIZE, LO_SIZE, tp_count), (CTX_HI, CTX_LO, "tp")
    )
    placed = (
        P("tp", CTX),
        P("tp", CTX),
        P("tp", CTX),
        P(None, "tp", None),
        P("tp", CTX, None),
        P(None, "tp"),
        P("tp", CTX),
    )
    return jax.shard_map(
        per_device,
        mesh=split_mesh,
        in_specs=placed,
        out_specs=(
            P("tp", CTX),
            P("tp", CTX),
            P("tp", CTX),
            P("tp", CTX),
            P("tp", CTX, None),
            P(CTX, "tp"),
        ),
        check_vma=False,
    )
```

```python
import math

import jax
import jax.numpy as jnp
from jax import lax
from jax.sharding import Mesh, PartitionSpec as P

BLOCK = 128
CTX_HI = "ctx_hi"
CTX_LO = "ctx_lo"
CTX = (CTX_HI, CTX_LO)
LO_SIZE = 8


TWO_PI = 2.0 * math.pi
DFT_PRECISION = lax.Precision.HIGH


def from_behind(value, axis, steps):
    count = lax.axis_size(axis)
    first, last = (max(0, -steps), min(count, count - steps))
    return lax.ppermute(value, axis, [(source, source + steps) for source in range(first, last)])


def fourier_table(count):
    element_indices = jnp.arange(count, dtype=jnp.int32)
    angles = (element_indices[:, None] * element_indices[None, :] % count).astype(jnp.float32) * (
        TWO_PI / count
    )
    return (jnp.cos(angles), -jnp.sin(angles))


def make_tables(length, block_width):
    row_count = 2 * length // block_width
    full_len = row_count * block_width
    outer_re, outer_im = fourier_table(row_count)
    inner_re, inner_im = fourier_table(block_width)
    row_index = jnp.arange(row_count, dtype=jnp.int32)[:, None]
    col_index = jnp.arange(block_width, dtype=jnp.int32)[None, :]
    angles = (row_index * col_index % full_len).astype(jnp.float32) * (TWO_PI / full_len)
    return (outer_re, outer_im, inner_re, inner_im, jnp.cos(angles), -jnp.sin(angles))


def spectrum(signal, tables):
    outer_re, outer_im, inner_re, inner_im, twist_re, twist_im = tables
    channels, length = signal.shape
    block_width = inner_re.shape[0]
    half_rows = length // block_width
    blocks = signal.reshape(channels, half_rows, block_width)
    section_re = jnp.einsum("kn,cnm->ckm", outer_re[:, :half_rows], blocks, precision=DFT_PRECISION)
    section_im = jnp.einsum("kn,cnm->ckm", outer_im[:, :half_rows], blocks, precision=DFT_PRECISION)
    turned_re = section_re * twist_re - section_im * twist_im
    turned_im = section_re * twist_im + section_im * twist_re
    frequency_real_component = jnp.matmul(turned_re, inner_re, precision=DFT_PRECISION) - jnp.matmul(
        turned_im, inner_im, precision=DFT_PRECISION
    )
    spec_im = jnp.matmul(turned_re, inner_im, precision=DFT_PRECISION) + jnp.matmul(
        turned_im, inner_re, precision=DFT_PRECISION
    )
    return (frequency_real_component, spec_im)


def inverse(frequency_real_component, spec_im, tables):
    outer_re, outer_im, inner_re, inner_im, twist_re, twist_im = tables
    channels, row_count, block_width = frequency_real_component.shape
    half_rows = row_count // 2
    back_re = jnp.matmul(frequency_real_component, inner_re, precision=DFT_PRECISION) + jnp.matmul(
        spec_im, inner_im, precision=DFT_PRECISION
    )
    back_im = jnp.matmul(spec_im, inner_re, precision=DFT_PRECISION) - jnp.matmul(
        frequency_real_component, inner_im, precision=DFT_PRECISION
    )
    turned_re = back_re * twist_re + back_im * twist_im
    turned_im = back_im * twist_re - back_re * twist_im
    signal = jnp.einsum("nk,ckm->cnm", outer_re[:half_rows], turned_re, precision=DFT_PRECISION)
    signal = signal + jnp.einsum("nk,ckm->cnm", outer_im[:half_rows], turned_im, precision=DFT_PRECISION)
    return (signal / (row_count * block_width)).reshape(channels, half_rows * block_width)


def causal_taps(stacked, earlier, weights):
    tap_count = weights.shape[2]
    length = stacked.shape[2]
    extended = jnp.concatenate([earlier, stacked], axis=2).astype(jnp.float32)
    running_total = jnp.zeros(stacked.shape, jnp.float32)
    for offset in range(tap_count):
        begin = tap_count - 1 - offset
        running_total = (
            running_total
            + weights[:, :, offset : offset + 1] * extended[:, :, begin : begin + length]
        )
    return running_total


def anticausal_taps(stacked, following, weights):
    tap_count = weights.shape[2]
    length = stacked.shape[2]
    extended = jnp.concatenate([stacked, following], axis=2).astype(jnp.float32)
    running_total = jnp.zeros(stacked.shape, jnp.float32)
    for offset in range(tap_count):
        running_total = (
            running_total
            + weights[:, :, offset : offset + 1] * extended[:, :, offset : offset + length]
        )
    return running_total


def to_channels(block):
    return lax.all_to_all(block, CTX, split_axis=0, concat_axis=1, tiled=True)


def to_positions(block):
    return lax.all_to_all(block, CTX, split_axis=1, concat_axis=0, tiled=True)


def swap_layouts(channel_block, position_block):
    count = lax.axis_size(CTX)
    channels, length = channel_block.shape
    local_len = length // count
    outgoing = jnp.stack(
        [
            channel_block.reshape(channels, count, local_len).transpose(1, 0, 2),
            position_block.reshape(count, channels, local_len),
        ],
        axis=1,
    )
    incoming = lax.all_to_all(outgoing, CTX, split_axis=0, concat_axis=0, tiled=True)
    positions = incoming[:, 0].reshape(count * channels, local_len)
    channels_out = incoming[:, 1].transpose(1, 0, 2).reshape(channels, length)
    return positions, channels_out


def weight_gradient(full_cotangent, gated_out):
    hi_count = lax.axis_size(CTX_HI)
    lo_count = lax.axis_size(CTX_LO)
    features, local_len = full_cotangent.shape
    rows = features // (hi_count * lo_count)
    group_gated = lax.all_gather(gated_out, CTX_LO, axis=1, tiled=True)
    group_gated = group_gated.reshape(gated_out.shape[0], lo_count, local_len)
    by_target = full_cotangent.reshape(hi_count, lo_count, rows, local_len).transpose(1, 0, 2, 3)
    group_rows = lax.all_to_all(by_target, CTX_LO, split_axis=0, concat_axis=0, tiled=True)
    weight_partial = lax.dot_general(
        group_rows, group_gated, (((0, 3), (1, 2)), ((), ())), preferred_element_type=jnp.float32
    ).astype(jnp.bfloat16)
    received = lax.all_to_all(weight_partial, CTX_HI, split_axis=0, concat_axis=0, tiled=True)
    return received.astype(jnp.float32).sum(0)


def per_device(query_in, key_in, value_in, short_weights, filters, out_weight, cotangent):
    tap_count = short_weights.shape[2]
    local_len = query_in.shape[1]
    stacked = jnp.stack([query_in, key_in, value_in])
    earlier = from_behind(stacked[:, :, local_len - (tap_count - 1) :], CTX, 1)
    shorts = causal_taps(stacked, earlier, short_weights).astype(jnp.bfloat16)
    product = (shorts[1].astype(jnp.float32) * shorts[2].astype(jnp.float32)).astype(jnp.bfloat16)
    product_chan = to_channels(product)
    tables = make_tables(product_chan.shape[1], BLOCK)
    channels = product_chan.shape[0]
    joint_re, joint_im = spectrum(
        jnp.concatenate([filters[0], product_chan.astype(jnp.float32)]), tables
    )
    kernel_re, product_re = joint_re[:channels], joint_re[channels:]
    kernel_im, product_im = joint_im[:channels], joint_im[channels:]
    convolved_chan = inverse(
        product_re * kernel_re - product_im * kernel_im,
        product_re * kernel_im + product_im * kernel_re,
        tables,
    ).astype(jnp.bfloat16)
    full_cotangent = lax.all_gather(cotangent, "tp", axis=0, tiled=True)
    grad_gated = lax.dot_general(
        out_weight, full_cotangent, (((0,), (0,)), ((), ())), preferred_element_type=jnp.float32
    )
    grad_conv = (grad_gated * shorts[0].astype(jnp.float32)).astype(jnp.bfloat16)
    convolved, grad_chan = swap_layouts(convolved_chan, grad_conv)
    gated_out = (shorts[0].astype(jnp.float32) * convolved.astype(jnp.float32)).astype(jnp.bfloat16)
    mixed_out = lax.psum_scatter(
        jnp.dot(out_weight, gated_out, preferred_element_type=jnp.float32).astype(jnp.bfloat16),
        "tp",
        scatter_dimension=0,
        tiled=True,
    )
    gated_for_weights, mixed_out = lax.optimization_barrier((gated_out, mixed_out))
    grad_out_weight = weight_gradient(full_cotangent, gated_for_weights)
    gradient_re, gradient_im = spectrum(grad_chan.astype(jnp.float32), tables)
    pair = inverse(
        jnp.concatenate(
            [
                kernel_re * gradient_re + kernel_im * gradient_im,
                product_re * gradient_re + product_im * gradient_im,
            ]
        ),
        jnp.concatenate(
            [
                kernel_re * gradient_im - kernel_im * gradient_re,
                product_re * gradient_im - product_im * gradient_re,
            ]
        ),
        tables,
    )
    grad_product_chan = pair[:channels].astype(jnp.bfloat16)
    grad_filters = pair[channels:].reshape(filters.shape)
    derivative_of_multiple = to_positions(grad_product_chan)
    grad_shorts = jnp.stack(
        [
            grad_gated * convolved.astype(jnp.float32),
            derivative_of_multiple.astype(jnp.float32) * shorts[2].astype(jnp.float32),
            derivative_of_multiple.astype(jnp.float32) * shorts[1].astype(jnp.float32),
        ]
    ).astype(jnp.bfloat16)
    following = from_behind(grad_shorts[:, :, : tap_count - 1], CTX, -1)
    gradients = anticausal_taps(grad_shorts, following, short_weights).astype(jnp.bfloat16)
    return (mixed_out, gradients[0], gradients[1], gradients[2], grad_filters, grad_out_weight)


def solution(mesh):
    ctx_count, tp_count = mesh.devices.shape
    split_mesh = Mesh(
        mesh.devices.reshape(ctx_count // LO_SIZE, LO_SIZE, tp_count), (CTX_HI, CTX_LO, "tp")
    )
    placed = (
        P("tp", CTX),
        P("tp", CTX),
        P("tp", CTX),
        P(None, "tp", None),
        P("tp", CTX, None),
        P(None, "tp"),
        P("tp", CTX),
    )
    return jax.shard_map(
        per_device,
        mesh=split_mesh,
        in_specs=placed,
        out_specs=(
            P("tp", CTX),
            P("tp", CTX),
            P("tp", CTX),
            P("tp", CTX),
            P("tp", CTX, None),
            P(CTX, "tp"),
        ),
        check_vma=False,
    )
```

```python
import math

import jax
import jax.numpy as jnp
from jax import lax
from jax.sharding import Mesh, PartitionSpec as P

BLOCK = 128
CTX_HI = "ctx_hi"
CTX_LO = "ctx_lo"
CTX = (CTX_HI, CTX_LO)
LO_SIZE = 8


TWO_PI = 2.0 * math.pi
DFT_PRECISION = lax.Precision.HIGH


def from_behind(value, axis, steps):
    count = lax.axis_size(axis)
    first, last = (max(0, -steps), min(count, count - steps))
    return lax.ppermute(value, axis, [(source, source + steps) for source in range(first, last)])


def fourier_table(count):
    element_indices = jnp.arange(count, dtype=jnp.int32)
    angles = (element_indices[:, None] * element_indices[None, :] % count).astype(jnp.float32) * (
        TWO_PI / count
    )
    return (jnp.cos(angles), -jnp.sin(angles))


def make_tables(length, block_width):
    row_count = 2 * length // block_width
    full_len = row_count * block_width
    outer_re, outer_im = fourier_table(row_count)
    inner_re, inner_im = fourier_table(block_width)
    row_index = jnp.arange(row_count, dtype=jnp.int32)[:, None]
    col_index = jnp.arange(block_width, dtype=jnp.int32)[None, :]
    angles = (row_index * col_index % full_len).astype(jnp.float32) * (TWO_PI / full_len)
    return (outer_re, outer_im, inner_re, inner_im, jnp.cos(angles), -jnp.sin(angles))


def spectrum(signal, tables):
    outer_re, outer_im, inner_re, inner_im, twist_re, twist_im = tables
    channels, length = signal.shape
    block_width = inner_re.shape[0]
    half_rows = length // block_width
    blocks = signal.reshape(channels, half_rows, block_width)
    section_re = jnp.einsum("kn,cnm->ckm", outer_re[:, :half_rows], blocks, precision=DFT_PRECISION)
    section_im = jnp.einsum("kn,cnm->ckm", outer_im[:, :half_rows], blocks, precision=DFT_PRECISION)
    turned_re = section_re * twist_re - section_im * twist_im
    turned_im = section_re * twist_im + section_im * twist_re
    frequency_real_component = jnp.matmul(turned_re, inner_re, precision=DFT_PRECISION) - jnp.matmul(
        turned_im, inner_im, precision=DFT_PRECISION
    )
    spec_im = jnp.matmul(turned_re, inner_im, precision=DFT_PRECISION) + jnp.matmul(
        turned_im, inner_re, precision=DFT_PRECISION
    )
    return (frequency_real_component, spec_im)


def inverse(frequency_real_component, spec_im, tables):
    outer_re, outer_im, inner_re, inner_im, twist_re, twist_im = tables
    channels, row_count, block_width = frequency_real_component.shape
    half_rows = row_count // 2
    back_re = jnp.matmul(frequency_real_component, inner_re, precision=DFT_PRECISION) + jnp.matmul(
        spec_im, inner_im, precision=DFT_PRECISION
    )
    back_im = jnp.matmul(spec_im, inner_re, precision=DFT_PRECISION) - jnp.matmul(
        frequency_real_component, inner_im, precision=DFT_PRECISION
    )
    turned_re = back_re * twist_re + back_im * twist_im
    turned_im = back_im * twist_re - back_re * twist_im
    signal = jnp.einsum("nk,ckm->cnm", outer_re[:half_rows], turned_re, precision=DFT_PRECISION)
    signal = signal + jnp.einsum("nk,ckm->cnm", outer_im[:half_rows], turned_im, precision=DFT_PRECISION)
    return (signal / (row_count * block_width)).reshape(channels, half_rows * block_width)


def causal_taps(stacked, earlier, weights):
    tap_count = weights.shape[2]
    length = stacked.shape[2]
    extended = jnp.concatenate([earlier, stacked], axis=2).astype(jnp.float32)
    running_total = jnp.zeros(stacked.shape, jnp.float32)
    for offset in range(tap_count):
        begin = tap_count - 1 - offset
        running_total = (
            running_total
            + weights[:, :, offset : offset + 1] * extended[:, :, begin : begin + length]
        )
    return running_total


def anticausal_taps(stacked, following, weights):
    tap_count = weights.shape[2]
    length = stacked.shape[2]
    extended = jnp.concatenate([stacked, following], axis=2).astype(jnp.float32)
    running_total = jnp.zeros(stacked.shape, jnp.float32)
    for offset in range(tap_count):
        running_total = (
            running_total
            + weights[:, :, offset : offset + 1] * extended[:, :, offset : offset + length]
        )
    return running_total


def to_channels(block):
    return lax.all_to_all(block, CTX, split_axis=0, concat_axis=1, tiled=True)


def to_positions(block):
    return lax.all_to_all(block, CTX, split_axis=1, concat_axis=0, tiled=True)


def swap_layouts(channel_block, position_block):
    count = lax.axis_size(CTX)
    channels, length = channel_block.shape
    local_len = length // count
    outgoing = jnp.stack(
        [
            channel_block.reshape(channels, count, local_len).transpose(1, 0, 2),
            position_block.reshape(count, channels, local_len),
        ],
        axis=1,
    )
    incoming = lax.all_to_all(outgoing, CTX, split_axis=0, concat_axis=0, tiled=True)
    positions = incoming[:, 0].reshape(count * channels, local_len)
    channels_out = incoming[:, 1].transpose(1, 0, 2).reshape(channels, length)
    return positions, channels_out


def weight_gradient(full_cotangent, gated_out):
    hi_count = lax.axis_size(CTX_HI)
    lo_count = lax.axis_size(CTX_LO)
    features, local_len = full_cotangent.shape
    rows = features // (hi_count * lo_count)
    by_target = full_cotangent.reshape(hi_count, lo_count, rows, local_len).transpose(1, 0, 2, 3)
    by_target = by_target.reshape(lo_count, hi_count * rows, local_len)
    outgoing = jnp.concatenate(
        [by_target, jnp.broadcast_to(gated_out, (lo_count,) + gated_out.shape)], axis=1
    )
    incoming = lax.all_to_all(outgoing, CTX_LO, split_axis=0, concat_axis=0, tiled=True)
    group_rows = incoming[:, : hi_count * rows]
    group_gated = incoming[:, hi_count * rows :]
    weight_partial = lax.dot_general(
        group_rows, group_gated, (((0, 2), (0, 2)), ((), ())), preferred_element_type=jnp.float32
    ).astype(jnp.bfloat16)
    weight_partial = weight_partial.reshape(hi_count, rows, gated_out.shape[0])
    received = lax.all_to_all(weight_partial, CTX_HI, split_axis=0, concat_axis=0, tiled=True)
    return received.astype(jnp.float32).sum(0)


def per_device(query_in, key_in, value_in, short_weights, filters, out_weight, cotangent):
    tap_count = short_weights.shape[2]
    local_len = query_in.shape[1]
    stacked = jnp.stack([query_in, key_in, value_in])
    earlier = from_behind(stacked[:, :, local_len - (tap_count - 1) :], CTX, 1)
    shorts = causal_taps(stacked, earlier, short_weights).astype(jnp.bfloat16)
    product = (shorts[1].astype(jnp.float32) * shorts[2].astype(jnp.float32)).astype(jnp.bfloat16)
    product_chan = to_channels(product)
    tables = make_tables(product_chan.shape[1], BLOCK)
    channels = product_chan.shape[0]
    joint_re, joint_im = spectrum(
        jnp.concatenate([filters[0], product_chan.astype(jnp.float32)]), tables
    )
    kernel_re, product_re = joint_re[:channels], joint_re[channels:]
    kernel_im, product_im = joint_im[:channels], joint_im[channels:]
    convolved_chan = inverse(
        product_re * kernel_re - product_im * kernel_im,
        product_re * kernel_im + product_im * kernel_re,
        tables,
    ).astype(jnp.bfloat16)
    full_cotangent = lax.all_gather(cotangent, "tp", axis=0, tiled=True)
    grad_gated = lax.dot_general(
        out_weight, full_cotangent, (((0,), (0,)), ((), ())), preferred_element_type=jnp.float32
    )
    grad_conv = (grad_gated * shorts[0].astype(jnp.float32)).astype(jnp.bfloat16)
    convolved, grad_chan = swap_layouts(convolved_chan, grad_conv)
    gated_out = (shorts[0].astype(jnp.float32) * convolved.astype(jnp.float32)).astype(jnp.bfloat16)
    mixed_out = lax.psum_scatter(
        jnp.dot(out_weight, gated_out, preferred_element_type=jnp.float32).astype(jnp.bfloat16),
        "tp",
        scatter_dimension=0,
        tiled=True,
    )
    grad_out_weight = weight_gradient(full_cotangent, gated_out)
    gradient_re, gradient_im = spectrum(grad_chan.astype(jnp.float32), tables)
    pair = inverse(
        jnp.concatenate(
            [
                kernel_re * gradient_re + kernel_im * gradient_im,
                product_re * gradient_re + product_im * gradient_im,
            ]
        ),
        jnp.concatenate(
            [
                kernel_re * gradient_im - kernel_im * gradient_re,
                product_re * gradient_im - product_im * gradient_re,
            ]
        ),
        tables,
    )
    grad_product_chan = pair[:channels].astype(jnp.bfloat16)
    grad_filters = pair[channels:].reshape(filters.shape)
    derivative_of_multiple = to_positions(grad_product_chan)
    grad_shorts = jnp.stack(
        [
            grad_gated * convolved.astype(jnp.float32),
            derivative_of_multiple.astype(jnp.float32) * shorts[2].astype(jnp.float32),
            derivative_of_multiple.astype(jnp.float32) * shorts[1].astype(jnp.float32),
        ]
    ).astype(jnp.bfloat16)
    following = from_behind(grad_shorts[:, :, : tap_count - 1], CTX, -1)
    gradients = anticausal_taps(grad_shorts, following, short_weights).astype(jnp.bfloat16)
    return (mixed_out, gradients[0], gradients[1], gradients[2], grad_filters, grad_out_weight)


def solution(mesh):
    ctx_count, tp_count = mesh.devices.shape
    split_mesh = Mesh(
        mesh.devices.reshape(ctx_count // LO_SIZE, LO_SIZE, tp_count), (CTX_HI, CTX_LO, "tp")
    )
    placed = (
        P("tp", CTX),
        P("tp", CTX),
        P("tp", CTX),
        P(None, "tp", None),
        P("tp", CTX, None),
        P(None, "tp"),
        P("tp", CTX),
    )
    return jax.shard_map(
        per_device,
        mesh=split_mesh,
        in_specs=placed,
        out_specs=(
            P("tp", CTX),
            P("tp", CTX),
            P("tp", CTX),
            P("tp", CTX),
            P("tp", CTX, None),
            P(CTX, "tp"),
        ),
        check_vma=False,
    )
```

```python
import math

import jax
import jax.numpy as jnp
from jax import lax
from jax.sharding import Mesh, PartitionSpec as P

BLOCK = 128
CTX_HI = "ctx_hi"
CTX_LO = "ctx_lo"
CTX = (CTX_HI, CTX_LO)
LO_SIZE = 8


TWO_PI = 2.0 * math.pi
DFT_PRECISION = lax.Precision.HIGH


def from_behind(value, axis, steps):
    count = lax.axis_size(axis)
    first, last = (max(0, -steps), min(count, count - steps))
    return lax.ppermute(value, axis, [(source, source + steps) for source in range(first, last)])


def fourier_table(count):
    element_indices = jnp.arange(count, dtype=jnp.int32)
    angles = (element_indices[:, None] * element_indices[None, :] % count).astype(jnp.float32) * (
        TWO_PI / count
    )
    return (jnp.cos(angles), -jnp.sin(angles))


def make_tables(length, block_width):
    row_count = 2 * length // block_width
    full_len = row_count * block_width
    outer_re, outer_im = fourier_table(row_count)
    inner_re, inner_im = fourier_table(block_width)
    row_index = jnp.arange(row_count, dtype=jnp.int32)[:, None]
    col_index = jnp.arange(block_width, dtype=jnp.int32)[None, :]
    angles = (row_index * col_index % full_len).astype(jnp.float32) * (TWO_PI / full_len)
    return (outer_re, outer_im, inner_re, inner_im, jnp.cos(angles), -jnp.sin(angles))


def spectrum(signal, tables):
    outer_re, outer_im, inner_re, inner_im, twist_re, twist_im = tables
    channels, length = signal.shape
    block_width = inner_re.shape[0]
    half_rows = length // block_width
    blocks = signal.reshape(channels, half_rows, block_width)
    section_re = jnp.einsum("kn,cnm->ckm", outer_re[:, :half_rows], blocks, precision=DFT_PRECISION)
    section_im = jnp.einsum("kn,cnm->ckm", outer_im[:, :half_rows], blocks, precision=DFT_PRECISION)
    turned_re = section_re * twist_re - section_im * twist_im
    turned_im = section_re * twist_im + section_im * twist_re
    frequency_real_component = jnp.matmul(turned_re, inner_re, precision=DFT_PRECISION) - jnp.matmul(
        turned_im, inner_im, precision=DFT_PRECISION
    )
    spec_im = jnp.matmul(turned_re, inner_im, precision=DFT_PRECISION) + jnp.matmul(
        turned_im, inner_re, precision=DFT_PRECISION
    )
    return (frequency_real_component, spec_im)


def inverse(frequency_real_component, spec_im, tables, precision=DFT_PRECISION):
    outer_re, outer_im, inner_re, inner_im, twist_re, twist_im = tables
    channels, row_count, block_width = frequency_real_component.shape
    half_rows = row_count // 2
    back_re = jnp.matmul(frequency_real_component, inner_re, precision=precision) + jnp.matmul(
        spec_im, inner_im, precision=precision
    )
    back_im = jnp.matmul(spec_im, inner_re, precision=precision) - jnp.matmul(
        frequency_real_component, inner_im, precision=precision
    )
    turned_re = back_re * twist_re + back_im * twist_im
    turned_im = back_im * twist_re - back_re * twist_im
    signal = jnp.einsum("nk,ckm->cnm", outer_re[:half_rows], turned_re, precision=precision)
    signal = signal + jnp.einsum("nk,ckm->cnm", outer_im[:half_rows], turned_im, precision=precision)
    return (signal / (row_count * block_width)).reshape(channels, half_rows * block_width)


def causal_taps(stacked, earlier, weights):
    tap_count = weights.shape[2]
    length = stacked.shape[2]
    extended = jnp.concatenate([earlier, stacked], axis=2).astype(jnp.float32)
    running_total = jnp.zeros(stacked.shape, jnp.float32)
    for offset in range(tap_count):
        begin = tap_count - 1 - offset
        running_total = (
            running_total
            + weights[:, :, offset : offset + 1] * extended[:, :, begin : begin + length]
        )
    return running_total


def anticausal_taps(stacked, following, weights):
    tap_count = weights.shape[2]
    length = stacked.shape[2]
    extended = jnp.concatenate([stacked, following], axis=2).astype(jnp.float32)
    running_total = jnp.zeros(stacked.shape, jnp.float32)
    for offset in range(tap_count):
        running_total = (
            running_total
            + weights[:, :, offset : offset + 1] * extended[:, :, offset : offset + length]
        )
    return running_total


def to_channels(block):
    return lax.all_to_all(block, CTX, split_axis=0, concat_axis=1, tiled=True)


def to_positions(block):
    return lax.all_to_all(block, CTX, split_axis=1, concat_axis=0, tiled=True)


def swap_layouts(channel_block, position_block):
    count = lax.axis_size(CTX)
    channels, length = channel_block.shape
    local_len = length // count
    outgoing = jnp.stack(
        [
            channel_block.reshape(channels, count, local_len).transpose(1, 0, 2),
            position_block.reshape(count, channels, local_len),
        ],
        axis=1,
    )
    incoming = lax.all_to_all(outgoing, CTX, split_axis=0, concat_axis=0, tiled=True)
    positions = incoming[:, 0].reshape(count * channels, local_len)
    channels_out = incoming[:, 1].transpose(1, 0, 2).reshape(channels, length)
    return positions, channels_out


def weight_gradient(full_cotangent, gated_out):
    hi_count = lax.axis_size(CTX_HI)
    lo_count = lax.axis_size(CTX_LO)
    features, local_len = full_cotangent.shape
    rows = features // (hi_count * lo_count)
    group_gated = lax.all_gather(gated_out, CTX_LO, axis=1, tiled=True)
    group_gated = group_gated.reshape(gated_out.shape[0], lo_count, local_len)
    by_target = full_cotangent.reshape(hi_count, lo_count, rows, local_len).transpose(1, 0, 2, 3)
    group_rows = lax.all_to_all(by_target, CTX_LO, split_axis=0, concat_axis=0, tiled=True)
    weight_partial = lax.dot_general(
        group_rows, group_gated, (((0, 3), (1, 2)), ((), ())), preferred_element_type=jnp.float32
    ).astype(jnp.bfloat16)
    received = lax.all_to_all(weight_partial, CTX_HI, split_axis=0, concat_axis=0, tiled=True)
    return received.astype(jnp.float32).sum(0)


def per_device(query_in, key_in, value_in, short_weights, filters, out_weight, cotangent):
    tap_count = short_weights.shape[2]
    local_len = query_in.shape[1]
    stacked = jnp.stack([query_in, key_in, value_in])
    earlier = from_behind(stacked[:, :, local_len - (tap_count - 1) :], CTX, 1)
    shorts = causal_taps(stacked, earlier, short_weights).astype(jnp.bfloat16)
    product = (shorts[1].astype(jnp.float32) * shorts[2].astype(jnp.float32)).astype(jnp.bfloat16)
    product_chan = to_channels(product)
    tables = make_tables(product_chan.shape[1], BLOCK)
    channels = product_chan.shape[0]
    joint_re, joint_im = spectrum(
        jnp.concatenate([filters[0], product_chan.astype(jnp.float32)]), tables
    )
    kernel_re, product_re = joint_re[:channels], joint_re[channels:]
    kernel_im, product_im = joint_im[:channels], joint_im[channels:]
    convolved_chan = inverse(
        product_re * kernel_re - product_im * kernel_im,
        product_re * kernel_im + product_im * kernel_re,
        tables,
        lax.Precision.DEFAULT,
    ).astype(jnp.bfloat16)
    full_cotangent = lax.all_gather(cotangent, "tp", axis=0, tiled=True)
    grad_gated = lax.dot_general(
        out_weight, full_cotangent, (((0,), (0,)), ((), ())), preferred_element_type=jnp.float32
    )
    grad_conv = (grad_gated * shorts[0].astype(jnp.float32)).astype(jnp.bfloat16)
    convolved, grad_chan = swap_layouts(convolved_chan, grad_conv)
    gated_out = (shorts[0].astype(jnp.float32) * convolved.astype(jnp.float32)).astype(jnp.bfloat16)
    mixed_out = lax.psum_scatter(
        jnp.dot(out_weight, gated_out, preferred_element_type=jnp.float32).astype(jnp.bfloat16),
        "tp",
        scatter_dimension=0,
        tiled=True,
    )
    grad_out_weight = weight_gradient(full_cotangent, gated_out)
    gradient_re, gradient_im = spectrum(grad_chan.astype(jnp.float32), tables)
    pair = inverse(
        jnp.concatenate(
            [
                kernel_re * gradient_re + kernel_im * gradient_im,
                product_re * gradient_re + product_im * gradient_im,
            ]
        ),
        jnp.concatenate(
            [
                kernel_re * gradient_im - kernel_im * gradient_re,
                product_re * gradient_im - product_im * gradient_re,
            ]
        ),
        tables,
    )
    grad_product_chan = pair[:channels].astype(jnp.bfloat16)
    grad_filters = pair[channels:].reshape(filters.shape)
    derivative_of_multiple = to_positions(grad_product_chan)
    grad_shorts = jnp.stack(
        [
            grad_gated * convolved.astype(jnp.float32),
            derivative_of_multiple.astype(jnp.float32) * shorts[2].astype(jnp.float32),
            derivative_of_multiple.astype(jnp.float32) * shorts[1].astype(jnp.float32),
        ]
    ).astype(jnp.bfloat16)
    following = from_behind(grad_shorts[:, :, : tap_count - 1], CTX, -1)
    gradients = anticausal_taps(grad_shorts, following, short_weights).astype(jnp.bfloat16)
    return (mixed_out, gradients[0], gradients[1], gradients[2], grad_filters, grad_out_weight)


def solution(mesh):
    ctx_count, tp_count = mesh.devices.shape
    split_mesh = Mesh(
        mesh.devices.reshape(ctx_count // LO_SIZE, LO_SIZE, tp_count), (CTX_HI, CTX_LO, "tp")
    )
    placed = (
        P("tp", CTX),
        P("tp", CTX),
        P("tp", CTX),
        P(None, "tp", None),
        P("tp", CTX, None),
        P(None, "tp"),
        P("tp", CTX),
    )
    return jax.shard_map(
        per_device,
        mesh=split_mesh,
        in_specs=placed,
        out_specs=(
            P("tp", CTX),
            P("tp", CTX),
            P("tp", CTX),
            P("tp", CTX),
            P("tp", CTX, None),
            P(CTX, "tp"),
        ),
        check_vma=False,
    )
```

```python
import math

import jax
import jax.numpy as jnp
from jax import lax
from jax.sharding import Mesh, PartitionSpec as P

BLOCK = 128
CTX_HI = "ctx_hi"
CTX_LO = "ctx_lo"
CTX = (CTX_HI, CTX_LO)
LO_SIZE = 8


TWO_PI = 2.0 * math.pi
DFT_PRECISION = lax.Precision.HIGH


def from_behind(value, axis, steps):
    count = lax.axis_size(axis)
    first, last = (max(0, -steps), min(count, count - steps))
    return lax.ppermute(value, axis, [(source, source + steps) for source in range(first, last)])


def fourier_table(count):
    element_indices = jnp.arange(count, dtype=jnp.int32)
    angles = (element_indices[:, None] * element_indices[None, :] % count).astype(jnp.float32) * (
        TWO_PI / count
    )
    return (jnp.cos(angles), -jnp.sin(angles))


def make_tables(length, block_width):
    row_count = 2 * length // block_width
    full_len = row_count * block_width
    outer_re, outer_im = fourier_table(row_count)
    inner_re, inner_im = fourier_table(block_width)
    row_index = jnp.arange(row_count, dtype=jnp.int32)[:, None]
    col_index = jnp.arange(block_width, dtype=jnp.int32)[None, :]
    angles = (row_index * col_index % full_len).astype(jnp.float32) * (TWO_PI / full_len)
    return (outer_re, outer_im, inner_re, inner_im, jnp.cos(angles), -jnp.sin(angles))


def spectrum(signal, tables):
    outer_re, outer_im, inner_re, inner_im, twist_re, twist_im = tables
    channels, length = signal.shape
    block_width = inner_re.shape[0]
    half_rows = length // block_width
    blocks = signal.reshape(channels, half_rows, block_width)
    section_re = jnp.einsum("kn,cnm->ckm", outer_re[:, :half_rows], blocks, precision=DFT_PRECISION)
    section_im = jnp.einsum("kn,cnm->ckm", outer_im[:, :half_rows], blocks, precision=DFT_PRECISION)
    turned_re = section_re * twist_re - section_im * twist_im
    turned_im = section_re * twist_im + section_im * twist_re
    frequency_real_component = jnp.matmul(turned_re, inner_re, precision=DFT_PRECISION) - jnp.matmul(
        turned_im, inner_im, precision=DFT_PRECISION
    )
    spec_im = jnp.matmul(turned_re, inner_im, precision=DFT_PRECISION) + jnp.matmul(
        turned_im, inner_re, precision=DFT_PRECISION
    )
    return (frequency_real_component, spec_im)


def inverse(frequency_real_component, spec_im, tables, precision=DFT_PRECISION):
    outer_re, outer_im, inner_re, inner_im, twist_re, twist_im = tables
    channels, row_count, block_width = frequency_real_component.shape
    half_rows = row_count // 2
    back_re = jnp.matmul(frequency_real_component, inner_re, precision=precision) + jnp.matmul(
        spec_im, inner_im, precision=precision
    )
    back_im = jnp.matmul(spec_im, inner_re, precision=precision) - jnp.matmul(
        frequency_real_component, inner_im, precision=precision
    )
    turned_re = back_re * twist_re + back_im * twist_im
    turned_im = back_im * twist_re - back_re * twist_im
    signal = jnp.einsum("nk,ckm->cnm", outer_re[:half_rows], turned_re, precision=precision)
    signal = signal + jnp.einsum("nk,ckm->cnm", outer_im[:half_rows], turned_im, precision=precision)
    return (signal / (row_count * block_width)).reshape(channels, half_rows * block_width)


def causal_taps(stacked, earlier, weights):
    tap_count = weights.shape[2]
    length = stacked.shape[2]
    extended = jnp.concatenate([earlier, stacked], axis=2).astype(jnp.float32)
    running_total = jnp.zeros(stacked.shape, jnp.float32)
    for offset in range(tap_count):
        begin = tap_count - 1 - offset
        running_total = (
            running_total
            + weights[:, :, offset : offset + 1] * extended[:, :, begin : begin + length]
        )
    return running_total


def anticausal_taps(stacked, following, weights):
    tap_count = weights.shape[2]
    length = stacked.shape[2]
    extended = jnp.concatenate([stacked, following], axis=2).astype(jnp.float32)
    running_total = jnp.zeros(stacked.shape, jnp.float32)
    for offset in range(tap_count):
        running_total = (
            running_total
            + weights[:, :, offset : offset + 1] * extended[:, :, offset : offset + length]
        )
    return running_total


def to_channels(block):
    return lax.all_to_all(block, CTX, split_axis=0, concat_axis=1, tiled=True)


def to_positions(block):
    return lax.all_to_all(block, CTX, split_axis=1, concat_axis=0, tiled=True)


def swap_layouts(channel_block, position_block):
    count = lax.axis_size(CTX)
    channels, length = channel_block.shape
    local_len = length // count
    outgoing = jnp.stack(
        [
            channel_block.reshape(channels, count, local_len).transpose(1, 0, 2),
            position_block.reshape(count, channels, local_len),
        ],
        axis=1,
    )
    incoming = lax.all_to_all(outgoing, CTX, split_axis=0, concat_axis=0, tiled=True)
    positions = incoming[:, 0].reshape(count * channels, local_len)
    channels_out = incoming[:, 1].transpose(1, 0, 2).reshape(channels, length)
    return positions, channels_out


def weight_gradient(full_cotangent, gated_out):
    hi_count = lax.axis_size(CTX_HI)
    lo_count = lax.axis_size(CTX_LO)
    features, local_len = full_cotangent.shape
    rows = features // (hi_count * lo_count)
    group_gated = lax.all_gather(gated_out, CTX_LO, axis=1, tiled=True)
    group_gated = group_gated.reshape(gated_out.shape[0], lo_count, local_len)
    by_target = full_cotangent.reshape(hi_count, lo_count, rows, local_len).transpose(1, 0, 2, 3)
    group_rows = lax.all_to_all(by_target, CTX_LO, split_axis=0, concat_axis=0, tiled=True)
    weight_partial = lax.dot_general(
        group_rows, group_gated, (((0, 3), (1, 2)), ((), ())), preferred_element_type=jnp.float32
    ).astype(jnp.bfloat16)
    received = lax.all_to_all(weight_partial, CTX_HI, split_axis=0, concat_axis=0, tiled=True)
    return received.astype(jnp.float32).sum(0)


def per_device(query_in, key_in, value_in, short_weights, filters, out_weight, cotangent):
    tap_count = short_weights.shape[2]
    local_len = query_in.shape[1]
    stacked = jnp.stack([query_in, key_in, value_in])
    earlier = from_behind(stacked[:, :, local_len - (tap_count - 1) :], CTX, 1)
    shorts = causal_taps(stacked, earlier, short_weights).astype(jnp.bfloat16)
    product = (shorts[1].astype(jnp.float32) * shorts[2].astype(jnp.float32)).astype(jnp.bfloat16)
    product_chan = to_channels(product)
    tables = make_tables(product_chan.shape[1], BLOCK)
    channels = product_chan.shape[0]
    joint_re, joint_im = spectrum(
        jnp.concatenate([filters[0], product_chan.astype(jnp.float32)]), tables
    )
    kernel_re, product_re = joint_re[:channels], joint_re[channels:]
    kernel_im, product_im = joint_im[:channels], joint_im[channels:]
    convolved_chan = inverse(
        product_re * kernel_re - product_im * kernel_im,
        product_re * kernel_im + product_im * kernel_re,
        tables,
        lax.Precision.DEFAULT,
    ).astype(jnp.bfloat16)
    full_cotangent = lax.all_gather(cotangent, "tp", axis=0, tiled=True)
    grad_gated = lax.dot_general(
        out_weight, full_cotangent, (((0,), (0,)), ((), ())), preferred_element_type=jnp.float32
    )
    grad_conv = (grad_gated * shorts[0].astype(jnp.float32)).astype(jnp.bfloat16)
    convolved, grad_chan = swap_layouts(convolved_chan, grad_conv)
    gated_out = (shorts[0].astype(jnp.float32) * convolved.astype(jnp.float32)).astype(jnp.bfloat16)
    mixed_out = lax.psum_scatter(
        jnp.dot(out_weight, gated_out, preferred_element_type=jnp.float32).astype(jnp.bfloat16),
        "tp",
        scatter_dimension=0,
        tiled=True,
    )
    grad_out_weight = weight_gradient(full_cotangent, gated_out)
    gradient_re, gradient_im = spectrum(grad_chan.astype(jnp.float32), tables)
    grad_product_chan = inverse(
        kernel_re * gradient_re + kernel_im * gradient_im,
        kernel_re * gradient_im - kernel_im * gradient_re,
        tables,
        lax.Precision.DEFAULT,
    ).astype(jnp.bfloat16)
    grad_filters = inverse(
        product_re * gradient_re + product_im * gradient_im,
        product_re * gradient_im - product_im * gradient_re,
        tables,
    ).reshape(filters.shape)
    derivative_of_multiple = to_positions(grad_product_chan)
    grad_shorts = jnp.stack(
        [
            grad_gated * convolved.astype(jnp.float32),
            derivative_of_multiple.astype(jnp.float32) * shorts[2].astype(jnp.float32),
            derivative_of_multiple.astype(jnp.float32) * shorts[1].astype(jnp.float32),
        ]
    ).astype(jnp.bfloat16)
    following = from_behind(grad_shorts[:, :, : tap_count - 1], CTX, -1)
    gradients = anticausal_taps(grad_shorts, following, short_weights).astype(jnp.bfloat16)
    return (mixed_out, gradients[0], gradients[1], gradients[2], grad_filters, grad_out_weight)


def solution(mesh):
    ctx_count, tp_count = mesh.devices.shape
    split_mesh = Mesh(
        mesh.devices.reshape(ctx_count // LO_SIZE, LO_SIZE, tp_count), (CTX_HI, CTX_LO, "tp")
    )
    placed = (
        P("tp", CTX),
        P("tp", CTX),
        P("tp", CTX),
        P(None, "tp", None),
        P("tp", CTX, None),
        P(None, "tp"),
        P("tp", CTX),
    )
    return jax.shard_map(
        per_device,
        mesh=split_mesh,
        in_specs=placed,
        out_specs=(
            P("tp", CTX),
            P("tp", CTX),
            P("tp", CTX),
            P("tp", CTX),
            P("tp", CTX, None),
            P(CTX, "tp"),
        ),
        check_vma=False,
    )
```

```python
import math

import jax
import jax.numpy as jnp
from jax import lax
from jax.sharding import Mesh, PartitionSpec as P

BLOCK = 128
CTX_HI = "ctx_hi"
CTX_LO = "ctx_lo"
CTX = (CTX_HI, CTX_LO)
LO_SIZE = 8


TWO_PI = 2.0 * math.pi
DFT_PRECISION = lax.Precision.HIGH


def from_behind(value, axis, steps):
    count = lax.axis_size(axis)
    first, last = (max(0, -steps), min(count, count - steps))
    return lax.ppermute(value, axis, [(source, source + steps) for source in range(first, last)])


def fourier_table(count):
    element_indices = jnp.arange(count, dtype=jnp.int32)
    angles = (element_indices[:, None] * element_indices[None, :] % count).astype(jnp.float32) * (
        TWO_PI / count
    )
    return (jnp.cos(angles), -jnp.sin(angles))


def make_tables(length, block_width):
    row_count = 2 * length // block_width
    full_len = row_count * block_width
    outer_re, outer_im = fourier_table(row_count)
    inner_re, inner_im = fourier_table(block_width)
    row_index = jnp.arange(row_count, dtype=jnp.int32)[:, None]
    col_index = jnp.arange(block_width, dtype=jnp.int32)[None, :]
    angles = (row_index * col_index % full_len).astype(jnp.float32) * (TWO_PI / full_len)
    return (outer_re, outer_im, inner_re, inner_im, jnp.cos(angles), -jnp.sin(angles))


def spectrum(signal, tables, precision=DFT_PRECISION):
    outer_re, outer_im, inner_re, inner_im, twist_re, twist_im = tables
    channels, length = signal.shape
    block_width = inner_re.shape[0]
    half_rows = length // block_width
    blocks = signal.reshape(channels, half_rows, block_width)
    section_re = jnp.einsum("kn,cnm->ckm", outer_re[:, :half_rows], blocks, precision=precision)
    section_im = jnp.einsum("kn,cnm->ckm", outer_im[:, :half_rows], blocks, precision=precision)
    turned_re = section_re * twist_re - section_im * twist_im
    turned_im = section_re * twist_im + section_im * twist_re
    frequency_real_component = jnp.matmul(turned_re, inner_re, precision=precision) - jnp.matmul(
        turned_im, inner_im, precision=precision
    )
    spec_im = jnp.matmul(turned_re, inner_im, precision=precision) + jnp.matmul(
        turned_im, inner_re, precision=precision
    )
    return (frequency_real_component, spec_im)


def inverse(frequency_real_component, spec_im, tables, precision=DFT_PRECISION):
    outer_re, outer_im, inner_re, inner_im, twist_re, twist_im = tables
    channels, row_count, block_width = frequency_real_component.shape
    half_rows = row_count // 2
    back_re = jnp.matmul(frequency_real_component, inner_re, precision=precision) + jnp.matmul(
        spec_im, inner_im, precision=precision
    )
    back_im = jnp.matmul(spec_im, inner_re, precision=precision) - jnp.matmul(
        frequency_real_component, inner_im, precision=precision
    )
    turned_re = back_re * twist_re + back_im * twist_im
    turned_im = back_im * twist_re - back_re * twist_im
    signal = jnp.einsum("nk,ckm->cnm", outer_re[:half_rows], turned_re, precision=precision)
    signal = signal + jnp.einsum("nk,ckm->cnm", outer_im[:half_rows], turned_im, precision=precision)
    return (signal / (row_count * block_width)).reshape(channels, half_rows * block_width)


def causal_taps(stacked, earlier, weights):
    tap_count = weights.shape[2]
    length = stacked.shape[2]
    extended = jnp.concatenate([earlier, stacked], axis=2).astype(jnp.float32)
    running_total = jnp.zeros(stacked.shape, jnp.float32)
    for offset in range(tap_count):
        begin = tap_count - 1 - offset
        running_total = (
            running_total
            + weights[:, :, offset : offset + 1] * extended[:, :, begin : begin + length]
        )
    return running_total


def anticausal_taps(stacked, following, weights):
    tap_count = weights.shape[2]
    length = stacked.shape[2]
    extended = jnp.concatenate([stacked, following], axis=2).astype(jnp.float32)
    running_total = jnp.zeros(stacked.shape, jnp.float32)
    for offset in range(tap_count):
        running_total = (
            running_total
            + weights[:, :, offset : offset + 1] * extended[:, :, offset : offset + length]
        )
    return running_total


def to_channels(block):
    return lax.all_to_all(block, CTX, split_axis=0, concat_axis=1, tiled=True)


def to_positions(block):
    return lax.all_to_all(block, CTX, split_axis=1, concat_axis=0, tiled=True)


def swap_layouts(channel_block, position_block):
    count = lax.axis_size(CTX)
    channels, length = channel_block.shape
    local_len = length // count
    outgoing = jnp.stack(
        [
            channel_block.reshape(channels, count, local_len).transpose(1, 0, 2),
            position_block.reshape(count, channels, local_len),
        ],
        axis=1,
    )
    incoming = lax.all_to_all(outgoing, CTX, split_axis=0, concat_axis=0, tiled=True)
    positions = incoming[:, 0].reshape(count * channels, local_len)
    channels_out = incoming[:, 1].transpose(1, 0, 2).reshape(channels, length)
    return positions, channels_out


def weight_gradient(full_cotangent, gated_out):
    hi_count = lax.axis_size(CTX_HI)
    lo_count = lax.axis_size(CTX_LO)
    features, local_len = full_cotangent.shape
    rows = features // (hi_count * lo_count)
    group_gated = lax.all_gather(gated_out, CTX_LO, axis=1, tiled=True)
    group_gated = group_gated.reshape(gated_out.shape[0], lo_count, local_len)
    by_target = full_cotangent.reshape(hi_count, lo_count, rows, local_len).transpose(1, 0, 2, 3)
    group_rows = lax.all_to_all(by_target, CTX_LO, split_axis=0, concat_axis=0, tiled=True)
    weight_partial = lax.dot_general(
        group_rows, group_gated, (((0, 3), (1, 2)), ((), ())), preferred_element_type=jnp.float32
    ).astype(jnp.bfloat16)
    received = lax.all_to_all(weight_partial, CTX_HI, split_axis=0, concat_axis=0, tiled=True)
    return received.astype(jnp.float32).sum(0)


def per_device(query_in, key_in, value_in, short_weights, filters, out_weight, cotangent):
    tap_count = short_weights.shape[2]
    local_len = query_in.shape[1]
    stacked = jnp.stack([query_in, key_in, value_in])
    earlier = from_behind(stacked[:, :, local_len - (tap_count - 1) :], CTX, 1)
    shorts = causal_taps(stacked, earlier, short_weights).astype(jnp.bfloat16)
    product = (shorts[1].astype(jnp.float32) * shorts[2].astype(jnp.float32)).astype(jnp.bfloat16)
    product_chan = to_channels(product)
    tables = make_tables(product_chan.shape[1], BLOCK)
    channels = product_chan.shape[0]
    joint_re, joint_im = spectrum(
        jnp.concatenate([filters[0], product_chan.astype(jnp.float32)]),
        tables,
        lax.Precision.DEFAULT,
    )
    kernel_re, product_re = joint_re[:channels], joint_re[channels:]
    kernel_im, product_im = joint_im[:channels], joint_im[channels:]
    convolved_chan = inverse(
        product_re * kernel_re - product_im * kernel_im,
        product_re * kernel_im + product_im * kernel_re,
        tables,
        lax.Precision.DEFAULT,
    ).astype(jnp.bfloat16)
    full_cotangent = lax.all_gather(cotangent, "tp", axis=0, tiled=True)
    grad_gated = lax.dot_general(
        out_weight, full_cotangent, (((0,), (0,)), ((), ())), preferred_element_type=jnp.float32
    )
    grad_conv = (grad_gated * shorts[0].astype(jnp.float32)).astype(jnp.bfloat16)
    convolved, grad_chan = swap_layouts(convolved_chan, grad_conv)
    gated_out = (shorts[0].astype(jnp.float32) * convolved.astype(jnp.float32)).astype(jnp.bfloat16)
    mixed_out = lax.psum_scatter(
        jnp.dot(out_weight, gated_out, preferred_element_type=jnp.float32).astype(jnp.bfloat16),
        "tp",
        scatter_dimension=0,
        tiled=True,
    )
    grad_out_weight = weight_gradient(full_cotangent, gated_out)
    gradient_re, gradient_im = spectrum(grad_chan.astype(jnp.float32), tables)
    pair = inverse(
        jnp.concatenate(
            [
                kernel_re * gradient_re + kernel_im * gradient_im,
                product_re * gradient_re + product_im * gradient_im,
            ]
        ),
        jnp.concatenate(
            [
                kernel_re * gradient_im - kernel_im * gradient_re,
                product_re * gradient_im - product_im * gradient_re,
            ]
        ),
        tables,
    )
    grad_product_chan = pair[:channels].astype(jnp.bfloat16)
    grad_filters = pair[channels:].reshape(filters.shape)
    derivative_of_multiple = to_positions(grad_product_chan)
    grad_shorts = jnp.stack(
        [
            grad_gated * convolved.astype(jnp.float32),
            derivative_of_multiple.astype(jnp.float32) * shorts[2].astype(jnp.float32),
            derivative_of_multiple.astype(jnp.float32) * shorts[1].astype(jnp.float32),
        ]
    ).astype(jnp.bfloat16)
    following = from_behind(grad_shorts[:, :, : tap_count - 1], CTX, -1)
    gradients = anticausal_taps(grad_shorts, following, short_weights).astype(jnp.bfloat16)
    return (mixed_out, gradients[0], gradients[1], gradients[2], grad_filters, grad_out_weight)


def solution(mesh):
    ctx_count, tp_count = mesh.devices.shape
    split_mesh = Mesh(
        mesh.devices.reshape(ctx_count // LO_SIZE, LO_SIZE, tp_count), (CTX_HI, CTX_LO, "tp")
    )
    placed = (
        P("tp", CTX),
        P("tp", CTX),
        P("tp", CTX),
        P(None, "tp", None),
        P("tp", CTX, None),
        P(None, "tp"),
        P("tp", CTX),
    )
    return jax.shard_map(
        per_device,
        mesh=split_mesh,
        in_specs=placed,
        out_specs=(
            P("tp", CTX),
            P("tp", CTX),
            P("tp", CTX),
            P("tp", CTX),
            P("tp", CTX, None),
            P(CTX, "tp"),
        ),
        check_vma=False,
    )
```

```python
import math

import jax
import jax.numpy as jnp
from jax import lax
from jax.sharding import Mesh, PartitionSpec as P

BLOCK = 128
CTX_HI = "ctx_hi"
CTX_LO = "ctx_lo"
CTX = (CTX_HI, CTX_LO)
LO_SIZE = 8


TWO_PI = 2.0 * math.pi
DFT_PRECISION = lax.Precision.HIGH


def from_behind(value, axis, steps):
    count = lax.axis_size(axis)
    first, last = (max(0, -steps), min(count, count - steps))
    return lax.ppermute(value, axis, [(source, source + steps) for source in range(first, last)])


def fourier_table(count):
    element_indices = jnp.arange(count, dtype=jnp.int32)
    angles = (element_indices[:, None] * element_indices[None, :] % count).astype(jnp.float32) * (
        TWO_PI / count
    )
    return (jnp.cos(angles), -jnp.sin(angles))


def make_tables(length, block_width):
    row_count = 2 * length // block_width
    full_len = row_count * block_width
    outer_re, outer_im = fourier_table(row_count)
    inner_re, inner_im = fourier_table(block_width)
    row_index = jnp.arange(row_count, dtype=jnp.int32)[:, None]
    col_index = jnp.arange(block_width, dtype=jnp.int32)[None, :]
    angles = (row_index * col_index % full_len).astype(jnp.float32) * (TWO_PI / full_len)
    return (outer_re, outer_im, inner_re, inner_im, jnp.cos(angles), -jnp.sin(angles))


def spectrum(signal, tables, precision=DFT_PRECISION):
    outer_re, outer_im, inner_re, inner_im, twist_re, twist_im = tables
    channels, length = signal.shape
    block_width = inner_re.shape[0]
    half_rows = length // block_width
    blocks = signal.reshape(channels, half_rows, block_width)
    section_re = jnp.einsum("kn,cnm->ckm", outer_re[:, :half_rows], blocks, precision=precision)
    section_im = jnp.einsum("kn,cnm->ckm", outer_im[:, :half_rows], blocks, precision=precision)
    turned_re = section_re * twist_re - section_im * twist_im
    turned_im = section_re * twist_im + section_im * twist_re
    frequency_real_component = jnp.matmul(turned_re, inner_re, precision=precision) - jnp.matmul(
        turned_im, inner_im, precision=precision
    )
    spec_im = jnp.matmul(turned_re, inner_im, precision=precision) + jnp.matmul(
        turned_im, inner_re, precision=precision
    )
    return (frequency_real_component, spec_im)


def inverse(frequency_real_component, spec_im, tables, precision=DFT_PRECISION):
    outer_re, outer_im, inner_re, inner_im, twist_re, twist_im = tables
    channels, row_count, block_width = frequency_real_component.shape
    half_rows = row_count // 2
    back_re = jnp.matmul(frequency_real_component, inner_re, precision=precision) + jnp.matmul(
        spec_im, inner_im, precision=precision
    )
    back_im = jnp.matmul(spec_im, inner_re, precision=precision) - jnp.matmul(
        frequency_real_component, inner_im, precision=precision
    )
    turned_re = back_re * twist_re + back_im * twist_im
    turned_im = back_im * twist_re - back_re * twist_im
    signal = jnp.einsum("nk,ckm->cnm", outer_re[:half_rows], turned_re, precision=precision)
    signal = signal + jnp.einsum("nk,ckm->cnm", outer_im[:half_rows], turned_im, precision=precision)
    return (signal / (row_count * block_width)).reshape(channels, half_rows * block_width)


def causal_taps(stacked, earlier, weights):
    tap_count = weights.shape[2]
    length = stacked.shape[2]
    extended = jnp.concatenate([earlier, stacked], axis=2).astype(jnp.float32)
    running_total = jnp.zeros(stacked.shape, jnp.float32)
    for offset in range(tap_count):
        begin = tap_count - 1 - offset
        running_total = (
            running_total
            + weights[:, :, offset : offset + 1] * extended[:, :, begin : begin + length]
        )
    return running_total


def anticausal_taps(stacked, following, weights):
    tap_count = weights.shape[2]
    length = stacked.shape[2]
    extended = jnp.concatenate([stacked, following], axis=2).astype(jnp.float32)
    running_total = jnp.zeros(stacked.shape, jnp.float32)
    for offset in range(tap_count):
        running_total = (
            running_total
            + weights[:, :, offset : offset + 1] * extended[:, :, offset : offset + length]
        )
    return running_total


def to_channels(block):
    return lax.all_to_all(block, CTX, split_axis=0, concat_axis=1, tiled=True)


def to_positions(block):
    return lax.all_to_all(block, CTX, split_axis=1, concat_axis=0, tiled=True)


def swap_layouts(channel_block, position_block):
    count = lax.axis_size(CTX)
    channels, length = channel_block.shape
    local_len = length // count
    outgoing = jnp.stack(
        [
            channel_block.reshape(channels, count, local_len).transpose(1, 0, 2),
            position_block.reshape(count, channels, local_len),
        ],
        axis=1,
    )
    incoming = lax.all_to_all(outgoing, CTX, split_axis=0, concat_axis=0, tiled=True)
    positions = incoming[:, 0].reshape(count * channels, local_len)
    channels_out = incoming[:, 1].transpose(1, 0, 2).reshape(channels, length)
    return positions, channels_out


def weight_gradient(full_cotangent, gated_out):
    hi_count = lax.axis_size(CTX_HI)
    lo_count = lax.axis_size(CTX_LO)
    features, local_len = full_cotangent.shape
    rows = features // (hi_count * lo_count)
    group_gated = lax.all_gather(gated_out, CTX_LO, axis=1, tiled=True)
    group_gated = group_gated.reshape(gated_out.shape[0], lo_count, local_len)
    by_target = full_cotangent.reshape(hi_count, lo_count, rows, local_len).transpose(1, 0, 2, 3)
    group_rows = lax.all_to_all(by_target, CTX_LO, split_axis=0, concat_axis=0, tiled=True)
    weight_partial = lax.dot_general(
        group_rows, group_gated, (((0, 3), (1, 2)), ((), ())), preferred_element_type=jnp.float32
    ).astype(jnp.bfloat16)
    received = lax.all_to_all(weight_partial, CTX_HI, split_axis=0, concat_axis=0, tiled=True)
    return received.astype(jnp.float32).sum(0)


def per_device(query_in, key_in, value_in, short_weights, filters, out_weight, cotangent):
    tap_count = short_weights.shape[2]
    local_len = query_in.shape[1]
    stacked = jnp.stack([query_in, key_in, value_in])
    earlier = from_behind(stacked[:, :, local_len - (tap_count - 1) :], CTX, 1)
    shorts = causal_taps(stacked, earlier, short_weights).astype(jnp.bfloat16)
    product = (shorts[1].astype(jnp.float32) * shorts[2].astype(jnp.float32)).astype(jnp.bfloat16)
    product_chan = to_channels(product)
    tables = make_tables(product_chan.shape[1], BLOCK)
    channels = product_chan.shape[0]
    joint_re, joint_im = spectrum(
        jnp.concatenate([filters[0], product_chan.astype(jnp.float32)]),
        tables,
        lax.Precision.DEFAULT,
    )
    kernel_re, product_re = joint_re[:channels], joint_re[channels:]
    kernel_im, product_im = joint_im[:channels], joint_im[channels:]
    convolved_chan = inverse(
        product_re * kernel_re - product_im * kernel_im,
        product_re * kernel_im + product_im * kernel_re,
        tables,
        lax.Precision.DEFAULT,
    ).astype(jnp.bfloat16)
    full_cotangent = lax.all_gather(cotangent, "tp", axis=0, tiled=True)
    grad_gated = lax.dot_general(
        out_weight, full_cotangent, (((0,), (0,)), ((), ())), preferred_element_type=jnp.float32
    )
    grad_conv = (grad_gated * shorts[0].astype(jnp.float32)).astype(jnp.bfloat16)
    convolved, grad_chan = swap_layouts(convolved_chan, grad_conv)
    gated_out = (shorts[0].astype(jnp.float32) * convolved.astype(jnp.float32)).astype(jnp.bfloat16)
    mixed_out = lax.psum_scatter(
        jnp.dot(out_weight, gated_out, preferred_element_type=jnp.float32).astype(jnp.bfloat16),
        "tp",
        scatter_dimension=0,
        tiled=True,
    )
    grad_out_weight = weight_gradient(full_cotangent, gated_out)
    gradient_re, gradient_im = spectrum(grad_chan.astype(jnp.float32), tables, lax.Precision.DEFAULT)
    pair = inverse(
        jnp.concatenate(
            [
                kernel_re * gradient_re + kernel_im * gradient_im,
                product_re * gradient_re + product_im * gradient_im,
            ]
        ),
        jnp.concatenate(
            [
                kernel_re * gradient_im - kernel_im * gradient_re,
                product_re * gradient_im - product_im * gradient_re,
            ]
        ),
        tables,
    )
    grad_product_chan = pair[:channels].astype(jnp.bfloat16)
    grad_filters = pair[channels:].reshape(filters.shape)
    derivative_of_multiple = to_positions(grad_product_chan)
    grad_shorts = jnp.stack(
        [
            grad_gated * convolved.astype(jnp.float32),
            derivative_of_multiple.astype(jnp.float32) * shorts[2].astype(jnp.float32),
            derivative_of_multiple.astype(jnp.float32) * shorts[1].astype(jnp.float32),
        ]
    ).astype(jnp.bfloat16)
    following = from_behind(grad_shorts[:, :, : tap_count - 1], CTX, -1)
    gradients = anticausal_taps(grad_shorts, following, short_weights).astype(jnp.bfloat16)
    return (mixed_out, gradients[0], gradients[1], gradients[2], grad_filters, grad_out_weight)


def solution(mesh):
    ctx_count, tp_count = mesh.devices.shape
    split_mesh = Mesh(
        mesh.devices.reshape(ctx_count // LO_SIZE, LO_SIZE, tp_count), (CTX_HI, CTX_LO, "tp")
    )
    placed = (
        P("tp", CTX),
        P("tp", CTX),
        P("tp", CTX),
        P(None, "tp", None),
        P("tp", CTX, None),
        P(None, "tp"),
        P("tp", CTX),
    )
    return jax.shard_map(
        per_device,
        mesh=split_mesh,
        in_specs=placed,
        out_specs=(
            P("tp", CTX),
            P("tp", CTX),
            P("tp", CTX),
            P("tp", CTX),
            P("tp", CTX, None),
            P(CTX, "tp"),
        ),
        check_vma=False,
    )
```
